128 devices in a mesh: chan: 8 (over y, core), pix: 16 (over x, z).
Axes of the slice: x: 4, y: 4, z: 4, core: 2. Of those that a mesh axis runs over, the one named last changes fastest.
Arguments:
- sky_cube: bfloat16 [512, 262144], P('chan', 'pix')
- beam_blocks: bfloat16 [512, 9, 128, 128], P('chan'), may hold values from -0.1875 to 0.1875
- pattern: int32 [512, 128, 9], P('chan'), may hold values from 0 to 127, as said below
- start_modes: float32 [512, 32], replicated, may hold values from -6 to 6
Outputs:
- cleaned: bfloat16 [512, 262144], P('chan', 'pix')
- mode_basis: float32 [512, 32], replicated
The draws below stay inside these ranges and needn't reach their ends.
Inputs may be any that keep to these rules, and one draw needn't show every extreme that they name: `pattern`: each source block is within 6 blocks of its output block, taken cyclically within the pixel group.
All inputs are finite; a program needn't handle non-finite values.
Results may differ from the reference program's by a relative error of at most 0.0062.
Values may be sent and summed in bfloat16 or wider, within the bound.
No kernel may reach another device: no remote copies, remote signals or barrier semaphores. Data moves between devices by JAX's collectives and lax.ppermute only.
A program may use at most 128 MiB of HBM per device.

```python
import math
import jax
import jax.numpy as jnp
from jax import lax

NCH = 512
BLK = 128
TAPS = 9
M_MAX = 32
ITERS = 3
NBLK = 128
NPIX = 262144
N_PIX = 16


def draw_sky_cube(key, part):
    keys = jax.random.split(key, 3)
    chan_scale = jnp.exp(jax.random.uniform(keys[1], (NCH, 1), jnp.float32) * math.log(10.0))
    ramp = 1.0 + 2.0 * jnp.arange(NPIX, dtype=jnp.float32) / NPIX
    pix_scale = jnp.exp(jax.random.uniform(keys[2], (1, NPIX), jnp.float32) * math.log(10.0)) * ramp[None, :]
    noise = jax.random.normal(keys[0], (NCH, NPIX), jnp.float32)
    values = noise * chan_scale * pix_scale / 12.0
    return values.astype(jnp.bfloat16)


def draw_pattern(key, part):
    offsets = jax.random.randint(key, (NCH, NBLK, TAPS), -2, 3)
    centre = jnp.arange(TAPS, dtype=jnp.int32) - TAPS // 2
    base = jnp.arange(NBLK, dtype=jnp.int32)[None, :, None] + centre[None, None, :]
    return jnp.mod(base + offsets, NBLK).astype(jnp.int32)


def shard_levels(stream_key, extent, cuts, smallest, largest):
    loudness = 1.0
    for axis_at, parts in cuts:
        draws = jax.random.uniform(jax.random.fold_in(jax.random.fold_in(stream_key, 6), axis_at), (parts,), jnp.float32, smallest / len(cuts), largest / len(cuts))
        loudness = loudness * jnp.repeat(jnp.exp(draws), extent[axis_at] // parts).reshape((-1,) + (1,) * (len(extent) - 1 - axis_at))
    return loudness


def normal_values(key, dims, scale, most, shards=(), kind=jnp.bfloat16):
    array = scale * jax.random.normal(key, dims, jnp.float32)
    if shards:
        array = array * shard_levels(key, dims, shards, -0.22, 0.18)
    return jnp.clip(array, -most, most).astype(kind)


def setup_inputs(seed: int = 0) -> dict:
    arg_keys = jax.random.split(jax.random.key(seed), 5)
    return {
        "sky_cube": draw_sky_cube(jax.random.fold_in(arg_keys[4], 71), 0),
        "beam_blocks": normal_values(arg_keys[1], (NCH, TAPS, BLK, BLK), (TAPS * BLK) ** -0.5, 0.1875, ((0, 8),)),
        "pattern": draw_pattern(jax.random.fold_in(arg_keys[4], 71), 0),
        "start_modes": normal_values(arg_keys[3], (NCH, M_MAX), 1.0, 6.0, (), jnp.float32),
    }


def smooth_channel(operands):
    channel_rows, channel_pattern, channel_beams = operands
    sources = channel_rows[:, channel_pattern]
    return jnp.einsum('gbkj,kij->gbi', sources.astype(jnp.float32), channel_beams.astype(jnp.float32)).astype(jnp.bfloat16)

def reference(sky_cube, beam_blocks, pattern, start_modes):
    tiles = sky_cube.reshape(NCH, N_PIX, NBLK, BLK)
    smoothed = lax.map(smooth_channel, (tiles, pattern, beam_blocks)).reshape(NCH, NPIX)
    gram = jnp.dot(smoothed.astype(jnp.float32), smoothed.T.astype(jnp.float32), preferred_element_type=jnp.float32) / NPIX
    basis = start_modes
    for sweep in range(ITERS):
        images = jnp.dot(gram, basis, precision=lax.Precision.HIGHEST)
        square = jnp.dot(images.T, images, precision=lax.Precision.HIGHEST)
        factor = jnp.linalg.cholesky(square)
        basis = lax.linalg.triangular_solve(factor, images, left_side=False, lower=True, transpose_a=True)
    mode_basis = basis
    modes_low = mode_basis.astype(jnp.bfloat16)
    coeffs = jnp.dot(modes_low.T.astype(jnp.float32), smoothed.astype(jnp.float32), preferred_element_type=jnp.float32).astype(jnp.bfloat16)
    cleaned = (smoothed.astype(jnp.float32) - jnp.dot(modes_low.astype(jnp.float32), coeffs.astype(jnp.float32), preferred_element_type=jnp.float32)).astype(jnp.bfloat16)
    return (cleaned, mode_basis)
```

```python
import numpy as np
import jax
import jax.numpy as jnp
from jax import lax
from jax.sharding import PartitionSpec as P

BLK = 128
ITERS = 3
AXES = ("chan", "pix")


def orthonormal(images):
    square = jnp.dot(images.T, images, precision=lax.Precision.HIGHEST)
    factor = jnp.linalg.cholesky(square)
    return lax.linalg.triangular_solve(
        factor, images, left_side=False, lower=True, transpose_a=True
    )


def sum_all(pieces):
    n = pieces.shape[0]
    got = lax.all_to_all(pieces, AXES, 0, 0, tiled=False)
    mine = jnp.sum(got, axis=0)
    spread = jnp.broadcast_to(mine[None], (n,) + mine.shape)
    return lax.all_to_all(spread, AXES, 0, 0, tiled=False)


def symmetric_sum(partial, nb):
    size = partial.shape[0]
    bs = size // nb
    upper = [(i, j) for i in range(nb) for j in range(i, nb)]
    blocks = partial.reshape(nb, bs, nb, bs).transpose(0, 2, 1, 3)
    iu = np.array([p[0] for p in upper])
    ju = np.array([p[1] for p in upper])
    packed = blocks[iu, ju].reshape(-1)
    n = lax.axis_size(AXES)
    total = packed.shape[0]
    width = -(-total // n)
    packed = jnp.pad(packed, (0, width * n - total))
    summed = sum_all(packed.reshape(n, width)).reshape(-1)[:total]
    summed = summed.reshape(len(upper), bs, bs)
    kmap = np.zeros((nb, nb), np.int32)
    for k, (i, j) in enumerate(upper):
        kmap[i, j] = k
        kmap[j, i] = k
    picked = summed[kmap]
    lower = np.array([[i > j for j in range(nb)] for i in range(nb)])
    full = jnp.where(lower[:, :, None, None], jnp.swapaxes(picked, -1, -2), picked)
    return full.transpose(0, 2, 1, 3).reshape(size, size)


def local(sky_cube, beam_blocks, pattern, start_modes):
    chans = sky_cube.shape[0]
    pix_group = sky_cube.shape[1]
    block_count = pix_group // BLK
    blocks = sky_cube.reshape(chans, block_count, BLK)
    block_ids = lax.broadcasted_iota(jnp.int32, (1, 1, 1, block_count), 3)
    selector = (pattern[:, :, :, None] == block_ids).astype(jnp.bfloat16)
    sources = jnp.einsum(
        "cbkn,cnj->cbkj", selector, blocks, preferred_element_type=jnp.float32
    ).astype(jnp.bfloat16)
    smoothed = jnp.einsum(
        "cbkj,ckij->cbi", sources, beam_blocks, preferred_element_type=jnp.float32
    ).astype(jnp.bfloat16)
    smoothed = smoothed.reshape(chans, pix_group)
    by_pixel = lax.all_to_all(smoothed, "chan", split_axis=1, concat_axis=0, tiled=True)
    n_chan = lax.axis_size("chan")
    all_pixels = pix_group * lax.axis_size("pix")
    basis = start_modes
    partial_value = jnp.dot(by_pixel, by_pixel.T, preferred_element_type=jnp.float32)
    total = symmetric_sum(partial_value, n_chan)
    gram = total / all_pixels
    for sweep in range(ITERS):
        images = jnp.dot(gram, basis, precision=lax.Precision.HIGHEST)
        basis = orthonormal(images)
    modes_low = basis.astype(jnp.bfloat16)
    coeffs = jnp.dot(modes_low.T, by_pixel, preferred_element_type=jnp.float32).astype(jnp.bfloat16)
    spread = jnp.broadcast_to(coeffs[None], (n_chan,) + coeffs.shape)
    gathered = lax.all_to_all(spread, "chan", 0, 0, tiled=False)
    all_coeffs = gathered.transpose(1, 0, 2).reshape(coeffs.shape[0], pix_group)
    me = lax.axis_index("chan")
    my_modes = lax.dynamic_slice_in_dim(modes_low, me * chans, chans, axis=0)
    removed = jnp.dot(my_modes, all_coeffs, preferred_element_type=jnp.float32)
    cleaned = (smoothed.astype(jnp.float32) - removed).astype(jnp.bfloat16)
    return (cleaned, basis)


def solution(mesh):
    return jax.shard_map(
        local,
        mesh=mesh,
        in_specs=(P("chan", "pix"), P("chan", None, None, None), P("chan", None, None), P()),
        out_specs=(P("chan", "pix"), P()),
        check_vma=False,
    )
```

```python
import jax
import jax.numpy as jnp
from jax import lax
from jax.sharding import PartitionSpec as P

BLK = 128
ITERS = 3
AXES = ("chan", "pix")


def orthonormal(images):
    square = jnp.dot(images.T, images, precision=lax.Precision.HIGHEST)
    factor = jnp.linalg.cholesky(square)
    return lax.linalg.triangular_solve(
        factor, images, left_side=False, lower=True, transpose_a=True
    )


def sum_all(pieces):
    n = pieces.shape[0]
    got = lax.all_to_all(pieces, AXES, 0, 0, tiled=False)
    mine = jnp.sum(got, axis=0)
    spread = jnp.broadcast_to(mine[None], (n,) + mine.shape)
    return lax.all_to_all(spread, AXES, 0, 0, tiled=False)


def symmetric_sum(partial, nb, scale):
    size = partial.shape[0]
    bs = size // nb
    rows = []
    for i in range(nb // 2):
        k = nb - 1 - i
        rows.append(jnp.concatenate(
            [partial[i * bs:(i + 1) * bs, i * bs:], partial[k * bs:(k + 1) * bs, k * bs:]], axis=1))
    packed = jnp.stack(rows)
    n = lax.axis_size(AXES)
    summed = sum_all(packed.reshape(n, -1)).reshape(packed.shape)
    upper = [None] * nb
    for i in range(nb // 2):
        k = nb - 1 - i
        width = (nb - i) * bs
        upper[i] = jnp.concatenate([jnp.zeros((bs, i * bs), jnp.float32), summed[i, :, :width]], axis=1)
        upper[k] = jnp.concatenate([jnp.zeros((bs, k * bs), jnp.float32), summed[i, :, width:]], axis=1)
    half = jnp.concatenate(upper, axis=0)
    blk = lax.broadcasted_iota(jnp.int32, (size, size), 0) // bs
    blk_t = lax.broadcasted_iota(jnp.int32, (size, size), 1) // bs
    return jnp.where(blk <= blk_t, half, half.T) * scale


def local(sky_cube, beam_blocks, pattern, start_modes):
    chans = sky_cube.shape[0]
    pix_group = sky_cube.shape[1]
    block_count = pix_group // BLK
    blocks = sky_cube.reshape(chans, block_count, BLK)
    block_ids = lax.broadcasted_iota(jnp.int32, (1, 1, 1, block_count), 3)
    selector = (pattern[:, :, :, None] == block_ids).astype(jnp.bfloat16)
    sources = jnp.einsum(
        "cbkn,cnj->cbkj", selector, blocks, preferred_element_type=jnp.float32
    ).astype(jnp.bfloat16)
    smoothed = jnp.einsum(
        "cbkj,ckij->cbi", sources, beam_blocks, preferred_element_type=jnp.float32
    ).astype(jnp.bfloat16)
    smoothed = smoothed.reshape(chans, pix_group)
    by_pixel = lax.all_to_all(smoothed, "chan", split_axis=1, concat_axis=0, tiled=True)
    n_chan = lax.axis_size("chan")
    all_pixels = pix_group * lax.axis_size("pix")
    basis = start_modes
    partial_value = jnp.dot(by_pixel, by_pixel.T, preferred_element_type=jnp.float32)
    gram = symmetric_sum(partial_value, n_chan, 1.0 / all_pixels)
    for sweep in range(ITERS):
        images = jnp.dot(gram, basis, precision=lax.Precision.HIGHEST)
        basis = orthonormal(images)
    modes_low = basis.astype(jnp.bfloat16)
    coeffs = jnp.dot(modes_low.T, by_pixel, preferred_element_type=jnp.float32).astype(jnp.bfloat16)
    spread = jnp.broadcast_to(coeffs[None], (n_chan,) + coeffs.shape)
    gathered = lax.all_to_all(spread, "chan", 0, 0, tiled=False)
    me = lax.axis_index("chan")
    my_modes = lax.dynamic_slice_in_dim(modes_low, me * chans, chans, axis=0)
    removed = jnp.einsum("cm,jmp->cjp", my_modes, gathered, preferred_element_type=jnp.float32)
    removed = removed.reshape(chans, pix_group)
    cleaned = (smoothed.astype(jnp.float32) - removed).astype(jnp.bfloat16)
    return (cleaned, basis)


def solution(mesh):
    return jax.shard_map(
        local,
        mesh=mesh,
        in_specs=(P("chan", "pix"), P("chan", None, None, None), P("chan", None, None), P()),
        out_specs=(P("chan", "pix"), P()),
        check_vma=False,
    )
```

```python
import jax
import jax.numpy as jnp
from jax import lax
from jax.sharding import PartitionSpec as P
from jax.experimental import pallas as pl

BLK = 128
ITERS = 3
AXES = ("chan", "pix")
CT = 4

def smooth_kernel(pat_ref, sky_ref, beam_ref, out_ref):
    taps = beam_ref.shape[1]
    nblk = sky_ref.shape[1]
    lane = lax.broadcasted_iota(jnp.int32, (nblk, nblk), 1)
    one = jnp.ones((nblk, nblk), jnp.float32)
    zero = jnp.zeros((nblk, nblk), jnp.float32)
    for c in range(sky_ref.shape[0]):
        p = pat_ref[c]
        sel = jnp.concatenate(
            [jnp.where(p[:, k:k + 1] == lane, one, zero).astype(jnp.bfloat16) for k in range(taps)], axis=0)
        src = jnp.dot(sel, sky_ref[c], preferred_element_type=jnp.float32).astype(jnp.bfloat16)
        lhs = jnp.concatenate([src[k * nblk:(k + 1) * nblk] for k in range(taps)], axis=1)
        rhs = jnp.concatenate([beam_ref[c, k] for k in range(taps)], axis=1)
        out = lax.dot_general(lhs, rhs, (((1,), (1,)), ((), ())), preferred_element_type=jnp.float32)
        out_ref[c] = out.astype(out_ref.dtype)

def smooth(sky3, beam, pattern):
    chans, nblk, blk = sky3.shape
    taps = beam.shape[1]
    return pl.pallas_call(
        smooth_kernel,
        out_shape=jax.ShapeDtypeStruct((chans, nblk, blk), jnp.bfloat16),
        grid=(chans // CT,),
        in_specs=[pl.BlockSpec((CT, nblk, taps), lambda i: (i, 0, 0)),
                  pl.BlockSpec((CT, nblk, blk), lambda i: (i, 0, 0)),
                  pl.BlockSpec((CT, taps, blk, blk), lambda i: (i, 0, 0, 0))],
        out_specs=pl.BlockSpec((CT, nblk, blk), lambda i: (i, 0, 0)),
    )(pattern, sky3, beam)


def orthonormal(images):
    square = jnp.dot(images.T, images, precision=lax.Precision.HIGHEST)
    factor = jnp.linalg.cholesky(square)
    return lax.linalg.triangular_solve(
        factor, images, left_side=False, lower=True, transpose_a=True
    )


def sum_all(pieces):
    n = pieces.shape[0]
    got = lax.all_to_all(pieces, AXES, 0, 0, tiled=False)
    mine = jnp.sum(got, axis=0)
    spread = jnp.broadcast_to(mine[None], (n,) + mine.shape)
    return lax.all_to_all(spread, AXES, 0, 0, tiled=False)


def symmetric_sum(partial, nb, scale):
    size = partial.shape[0]
    bs = size // nb
    rows = []
    for i in range(nb // 2):
        k = nb - 1 - i
        rows.append(jnp.concatenate(
            [partial[i * bs:(i + 1) * bs, i * bs:], partial[k * bs:(k + 1) * bs, k * bs:]], axis=1))
    packed = jnp.stack(rows)
    n = lax.axis_size(AXES)
    summed = sum_all(packed.reshape(n, -1)).reshape(packed.shape)
    upper = [None] * nb
    for i in range(nb // 2):
        k = nb - 1 - i
        width = (nb - i) * bs
        upper[i] = jnp.concatenate([jnp.zeros((bs, i * bs), jnp.float32), summed[i, :, :width]], axis=1)
        upper[k] = jnp.concatenate([jnp.zeros((bs, k * bs), jnp.float32), summed[i, :, width:]], axis=1)
    half = jnp.concatenate(upper, axis=0)
    blk = lax.broadcasted_iota(jnp.int32, (size, size), 0) // bs
    blk_t = lax.broadcasted_iota(jnp.int32, (size, size), 1) // bs
    return jnp.where(blk <= blk_t, half, half.T) * scale


def local(sky_cube, beam_blocks, pattern, start_modes):
    chans = sky_cube.shape[0]
    pix_group = sky_cube.shape[1]
    block_count = pix_group // BLK
    blocks = sky_cube.reshape(chans, block_count, BLK)
    smoothed = smooth(blocks, beam_blocks, pattern)
    smoothed = smoothed.reshape(chans, pix_group)
    by_pixel = lax.all_to_all(smoothed, "chan", split_axis=1, concat_axis=0, tiled=True)
    n_chan = lax.axis_size("chan")
    all_pixels = pix_group * lax.axis_size("pix")
    basis = start_modes
    partial_value = jnp.dot(by_pixel, by_pixel.T, preferred_element_type=jnp.float32)
    gram = symmetric_sum(partial_value, n_chan, 1.0 / all_pixels)
    for sweep in range(ITERS):
        images = jnp.dot(gram, basis, precision=lax.Precision.HIGHEST)
        basis = orthonormal(images)
    modes_low = basis.astype(jnp.bfloat16)
    coeffs = jnp.dot(modes_low.T, by_pixel, preferred_element_type=jnp.float32).astype(jnp.bfloat16)
    spread = jnp.broadcast_to(coeffs[None], (n_chan,) + coeffs.shape)
    gathered = lax.all_to_all(spread, "chan", 0, 0, tiled=False)
    me = lax.axis_index("chan")
    my_modes = lax.dynamic_slice_in_dim(modes_low, me * chans, chans, axis=0)
    removed = jnp.einsum("cm,jmp->cjp", my_modes, gathered, preferred_element_type=jnp.float32)
    removed = removed.reshape(chans, pix_group)
    cleaned = (smoothed.astype(jnp.float32) - removed).astype(jnp.bfloat16)
    return (cleaned, basis)


def solution(mesh):
    return jax.shard_map(
        local,
        mesh=mesh,
        in_specs=(P("chan", "pix"), P("chan", None, None, None), P("chan", None, None), P()),
        out_specs=(P("chan", "pix"), P()),
        check_vma=False,
    )
```

```python
import jax
import jax.numpy as jnp
from jax import lax
from jax.sharding import PartitionSpec as P
from jax.experimental import pallas as pl

BLK = 128
ITERS = 3
AXES = ("chan", "pix")
CT = 8

def smooth_kernel(pat_ref, sky_ref, beam_ref, out_ref):
    taps = beam_ref.shape[1]
    nblk = sky_ref.shape[1]
    lane = lax.broadcasted_iota(jnp.int32, (nblk, nblk), 1)
    one = jnp.ones((nblk, nblk), jnp.float32)
    zero = jnp.zeros((nblk, nblk), jnp.float32)
    for c in range(sky_ref.shape[0]):
        p = pat_ref[c]
        sel = jnp.concatenate(
            [jnp.where(p[:, k:k + 1] == lane, one, zero).astype(jnp.bfloat16) for k in range(taps)], axis=0)
        src = jnp.dot(sel, sky_ref[c], preferred_element_type=jnp.float32).astype(jnp.bfloat16)
        lhs = jnp.concatenate([src[k * nblk:(k + 1) * nblk] for k in range(taps)], axis=1)
        rhs = jnp.concatenate([beam_ref[c, k] for k in range(taps)], axis=1)
        out = lax.dot_general(lhs, rhs, (((1,), (1,)), ((), ())), preferred_element_type=jnp.float32)
        out_ref[:, c] = out.astype(out_ref.dtype).reshape(out_ref.shape[0], out_ref.shape[2], out_ref.shape[3])

def smooth(sky3, beam, pattern, parts):
    chans, nblk, blk = sky3.shape
    taps = beam.shape[1]
    return pl.pallas_call(
        smooth_kernel,
        out_shape=jax.ShapeDtypeStruct((parts, chans, nblk // parts, blk), jnp.bfloat16),
        grid=(chans // CT,),
        in_specs=[pl.BlockSpec((CT, nblk, taps), lambda i: (i, 0, 0)),
                  pl.BlockSpec((CT, nblk, blk), lambda i: (i, 0, 0)),
                  pl.BlockSpec((CT, taps, blk, blk), lambda i: (i, 0, 0, 0))],
        out_specs=pl.BlockSpec((parts, CT, nblk // parts, blk), lambda i: (0, i, 0, 0)),
    )(pattern, sky3, beam)


def orthonormal(images):
    square = jnp.dot(images.T, images, precision=lax.Precision.HIGHEST)
    factor = jnp.linalg.cholesky(square)
    return lax.linalg.triangular_solve(
        factor, images, left_side=False, lower=True, transpose_a=True
    )


def sum_all(pieces):
    n = pieces.shape[0]
    got = lax.all_to_all(pieces, AXES, 0, 0, tiled=False)
    mine = jnp.sum(got, axis=0)
    spread = jnp.broadcast_to(mine[None], (n,) + mine.shape)
    return lax.all_to_all(spread, AXES, 0, 0, tiled=False)


def symmetric_sum(partial, nb, scale):
    size = partial.shape[0]
    bs = size // nb
    rows = []
    for i in range(nb // 2):
        k = nb - 1 - i
        rows.append(jnp.concatenate(
            [partial[i * bs:(i + 1) * bs, i * bs:], partial[k * bs:(k + 1) * bs, k * bs:]], axis=1))
    packed = jnp.stack(rows)
    n = lax.axis_size(AXES)
    summed = sum_all(packed.reshape(n, -1)).reshape(packed.shape)
    upper = [None] * nb
    for i in range(nb // 2):
        k = nb - 1 - i
        width = (nb - i) * bs
        upper[i] = jnp.concatenate([jnp.zeros((bs, i * bs), jnp.float32), summed[i, :, :width]], axis=1)
        upper[k] = jnp.concatenate([jnp.zeros((bs, k * bs), jnp.float32), summed[i, :, width:]], axis=1)
    half = jnp.concatenate(upper, axis=0)
    blk = lax.broadcasted_iota(jnp.int32, (size, size), 0) // bs
    blk_t = lax.broadcasted_iota(jnp.int32, (size, size), 1) // bs
    return jnp.where(blk <= blk_t, half, half.T) * scale


def local(sky_cube, beam_blocks, pattern, start_modes):
    chans = sky_cube.shape[0]
    pix_group = sky_cube.shape[1]
    block_count = pix_group // BLK
    blocks = sky_cube.reshape(chans, block_count, BLK)
    n_chan = lax.axis_size("chan")
    chunks = smooth(blocks, beam_blocks, pattern, n_chan).reshape(n_chan, chans, pix_group // n_chan)
    by_pixel = lax.all_to_all(chunks, "chan", 0, 0, tiled=True).reshape(n_chan * chans, pix_group // n_chan)
    all_pixels = pix_group * lax.axis_size("pix")
    basis = start_modes
    partial_value = jnp.dot(by_pixel, by_pixel.T, preferred_element_type=jnp.float32)
    gram = symmetric_sum(partial_value, n_chan, 1.0 / all_pixels)
    for sweep in range(ITERS):
        images = jnp.dot(gram, basis, precision=lax.Precision.HIGHEST)
        basis = orthonormal(images)
    modes_low = basis.astype(jnp.bfloat16)
    coeffs = jnp.dot(modes_low.T, by_pixel, preferred_element_type=jnp.float32).astype(jnp.bfloat16)
    spread = jnp.broadcast_to(coeffs[None], (n_chan,) + coeffs.shape)
    gathered = lax.all_to_all(spread, "chan", 0, 0, tiled=False)
    me = lax.axis_index("chan")
    my_modes = lax.dynamic_slice_in_dim(modes_low, me * chans, chans, axis=0)
    removed = jnp.einsum("cm,jmp->jcp", my_modes, gathered, preferred_element_type=jnp.float32)
    cleaned = (chunks.astype(jnp.float32) - removed).astype(jnp.bfloat16)
    cleaned = cleaned.transpose(1, 0, 2).reshape(chans, pix_group)
    return (cleaned, basis)


def solution(mesh):
    return jax.shard_map(
        local,
        mesh=mesh,
        in_specs=(P("chan", "pix"), P("chan", None, None, None), P("chan", None, None), P()),
        out_specs=(P("chan", "pix"), P()),
        check_vma=False,
    )
```

```python
import jax
import jax.numpy as jnp
from jax import lax
from jax.sharding import PartitionSpec as P
from jax.experimental import pallas as pl

BLK = 128
ITERS = 3
AXES = ("chan", "pix")
CT = 8

def smooth_kernel(pat_ref, sky_ref, beam_ref, out_ref):
    taps = beam_ref.shape[1]
    nblk = sky_ref.shape[1]
    lane = lax.broadcasted_iota(jnp.int32, (nblk, nblk), 1).astype(jnp.float32)
    row = lax.broadcasted_iota(jnp.int32, (nblk, nblk), 0)
    eye = jnp.where(row == lax.broadcasted_iota(jnp.int32, (nblk, nblk), 1), 1.0, 0.0).astype(jnp.bfloat16)
    one = jnp.ones((nblk, nblk), jnp.float32)
    zero = jnp.zeros((nblk, nblk), jnp.float32)
    for c in range(sky_ref.shape[0]):
        p = pat_ref[:, c, :].astype(jnp.float32).astype(jnp.bfloat16)
        p = lax.dot_general(eye, p, (((1,), (1,)), ((), ())), preferred_element_type=jnp.float32)
        sel = jnp.concatenate(
            [jnp.where(p[:, k:k + 1] == lane, one, zero).astype(jnp.bfloat16) for k in range(taps)], axis=0)
        src = jnp.dot(sel, sky_ref[c], preferred_element_type=jnp.float32).astype(jnp.bfloat16)
        lhs = jnp.concatenate([src[k * nblk:(k + 1) * nblk] for k in range(taps)], axis=1)
        rhs = jnp.concatenate([beam_ref[c, k] for k in range(taps)], axis=1)
        out = lax.dot_general(lhs, rhs, (((1,), (1,)), ((), ())), preferred_element_type=jnp.float32)
        out_ref[:, c] = out.astype(out_ref.dtype).reshape(out_ref.shape[0], out_ref.shape[2], out_ref.shape[3])

def smooth(sky3, beam, pattern, parts):
    chans, nblk, blk = sky3.shape
    taps = beam.shape[1]
    pat_t = jnp.transpose(pattern, (2, 0, 1))
    return pl.pallas_call(
        smooth_kernel,
        out_shape=jax.ShapeDtypeStruct((parts, chans, nblk // parts, blk), jnp.bfloat16),
        grid=(chans // CT,),
        in_specs=[pl.BlockSpec((taps, CT, nblk), lambda i: (0, i, 0)),
                  pl.BlockSpec((CT, nblk, blk), lambda i: (i, 0, 0)),
                  pl.BlockSpec((CT, taps, blk, blk), lambda i: (i, 0, 0, 0))],
        out_specs=pl.BlockSpec((parts, CT, nblk // parts, blk), lambda i: (0, i, 0, 0)),
    )(pat_t, sky3, beam)


def orthonormal(images):
    square = jnp.dot(images.T, images, precision=lax.Precision.HIGHEST)
    factor = jnp.linalg.cholesky(square)
    return lax.linalg.triangular_solve(
        factor, images, left_side=False, lower=True, transpose_a=True
    )


def sum_all(pieces):
    n = pieces.shape[0]
    got = lax.all_to_all(pieces, AXES, 0, 0, tiled=False)
    mine = jnp.sum(got, axis=0)
    spread = jnp.broadcast_to(mine[None], (n,) + mine.shape)
    return lax.all_to_all(spread, AXES, 0, 0, tiled=False)


def symmetric_sum(partial, nb, scale):
    size = partial.shape[0]
    bs = size // nb
    rows = []
    for i in range(nb // 2):
        k = nb - 1 - i
        rows.append(jnp.concatenate(
            [partial[i * bs:(i + 1) * bs, i * bs:], partial[k * bs:(k + 1) * bs, k * bs:]], axis=1))
    packed = jnp.stack(rows)
    n = lax.axis_size(AXES)
    summed = sum_all(packed.reshape(n, -1)).reshape(packed.shape)
    lead = (nb // 2 - 1) * bs
    padded = jnp.pad(summed, ((0, 0), (0, 0), (lead, 0)))
    width = padded.shape[2]
    upper = []
    for r in range(nb):
        if r < nb // 2:
            start = lead - r * bs
            upper.append(padded[r, :, start:start + size])
        else:
            upper.append(padded[nb - 1 - r, :, width - size:])
    half = jnp.concatenate(upper, axis=0)
    blk = lax.broadcasted_iota(jnp.int32, (size, size), 0) // bs
    blk_t = lax.broadcasted_iota(jnp.int32, (size, size), 1) // bs
    return jnp.where(blk <= blk_t, half, half.T) * scale


def local(sky_cube, beam_blocks, pattern, start_modes):
    chans = sky_cube.shape[0]
    pix_group = sky_cube.shape[1]
    block_count = pix_group // BLK
    blocks = sky_cube.reshape(chans, block_count, BLK)
    n_chan = lax.axis_size("chan")
    chunks = smooth(blocks, beam_blocks, pattern, n_chan)
    by_pixel = lax.all_to_all(chunks, "chan", 0, 0, tiled=True)
    by_pixel = by_pixel.reshape((n_chan * chans,) + by_pixel.shape[2:])
    all_pixels = pix_group * lax.axis_size("pix")
    basis = start_modes
    partial_value = lax.dot_general(
        by_pixel, by_pixel, (((1, 2), (1, 2)), ((), ())), preferred_element_type=jnp.float32)
    gram = symmetric_sum(partial_value, n_chan, 1.0 / all_pixels)
    for sweep in range(ITERS):
        images = jnp.dot(gram, basis, precision=lax.Precision.HIGHEST)
        basis = orthonormal(images)
    modes_low = basis.astype(jnp.bfloat16)
    coeffs = jnp.einsum("cm,cbi->mbi", modes_low, by_pixel, preferred_element_type=jnp.float32).astype(jnp.bfloat16)
    spread = jnp.broadcast_to(coeffs[None], (n_chan,) + coeffs.shape)
    gathered = lax.all_to_all(spread, "chan", 0, 0, tiled=False)
    me = lax.axis_index("chan")
    my_modes = lax.dynamic_slice_in_dim(modes_low, me * chans, chans, axis=0)
    removed = jnp.einsum("cm,jmbi->cjbi", my_modes, gathered, preferred_element_type=jnp.float32)
    cleaned = (chunks.transpose(1, 0, 2, 3).astype(jnp.float32) - removed).astype(jnp.bfloat16)
    cleaned = cleaned.reshape(chans, pix_group)
    return (cleaned, basis)


def solution(mesh):
    return jax.shard_map(
        local,
        mesh=mesh,
        in_specs=(P("chan", "pix"), P("chan", None, None, None), P("chan", None, None), P()),
        out_specs=(P("chan", "pix"), P()),
        check_vma=False,
    )
```

```python
import jax
import jax.numpy as jnp
from jax import lax
from jax.sharding import PartitionSpec as P
from jax.experimental import pallas as pl

BLK = 128
ITERS = 3
AXES = ("chan", "pix")
CT = 8

def smooth_kernel(pat_ref, sky_ref, beam_ref, out_ref):
    taps = beam_ref.shape[1]
    nblk = sky_ref.shape[1]
    lane = lax.broadcasted_iota(jnp.int32, (nblk, nblk), 1).astype(jnp.float32)
    row = lax.broadcasted_iota(jnp.int32, (nblk, nblk), 0)
    eye = jnp.where(row == lax.broadcasted_iota(jnp.int32, (nblk, nblk), 1), 1.0, 0.0).astype(jnp.bfloat16)
    one = jnp.ones((nblk, nblk), jnp.float32)
    zero = jnp.zeros((nblk, nblk), jnp.float32)
    ct = sky_ref.shape[0]
    pat = pat_ref[...].reshape(taps * ct, nblk).astype(jnp.float32).astype(jnp.bfloat16)
    pat = lax.dot_general(eye, pat, (((1,), (1,)), ((), ())), preferred_element_type=jnp.float32)
    for c in range(ct):
        sel = jnp.concatenate(
            [jnp.where(pat[:, k * ct + c:k * ct + c + 1] == lane, one, zero).astype(jnp.bfloat16)
             for k in range(taps)], axis=0)
        src = jnp.dot(sel, sky_ref[c], preferred_element_type=jnp.float32).astype(jnp.bfloat16)
        lhs = jnp.concatenate([src[k * nblk:(k + 1) * nblk] for k in range(taps)], axis=1)
        rhs = jnp.concatenate([beam_ref[c, k] for k in range(taps)], axis=1)
        out = lax.dot_general(lhs, rhs, (((1,), (1,)), ((), ())), preferred_element_type=jnp.float32)
        out_ref[:, c] = out.astype(out_ref.dtype).reshape(out_ref.shape[0], out_ref.shape[2], out_ref.shape[3])

def smooth(sky3, beam, pattern, parts):
    chans, nblk, blk = sky3.shape
    taps = beam.shape[1]
    pat_t = jnp.transpose(pattern, (2, 0, 1))
    return pl.pallas_call(
        smooth_kernel,
        out_shape=jax.ShapeDtypeStruct((parts, chans, nblk // parts, blk), jnp.bfloat16),
        grid=(chans // CT,),
        in_specs=[pl.BlockSpec((taps, CT, nblk), lambda i: (0, i, 0)),
                  pl.BlockSpec((CT, nblk, blk), lambda i: (i, 0, 0)),
                  pl.BlockSpec((CT, taps, blk, blk), lambda i: (i, 0, 0, 0))],
        out_specs=pl.BlockSpec((parts, CT, nblk // parts, blk), lambda i: (0, i, 0, 0)),
    )(pat_t, sky3, beam)


def orthonormal(images):
    square = jnp.dot(images.T, images, precision=lax.Precision.HIGHEST)
    factor = jnp.linalg.cholesky(square)
    return lax.linalg.triangular_solve(
        factor, images, left_side=False, lower=True, transpose_a=True
    )


def sum_all(pieces):
    n = pieces.shape[0]
    got = lax.all_to_all(pieces, AXES, 0, 0, tiled=False)
    mine = jnp.sum(got, axis=0)
    spread = jnp.broadcast_to(mine[None], (n,) + mine.shape)
    return lax.all_to_all(spread, AXES, 0, 0, tiled=False)


def symmetric_sum(partial, nb, scale):
    size = partial.shape[0]
    bs = size // nb
    rows = []
    for i in range(nb // 2):
        k = nb - 1 - i
        rows.append(jnp.concatenate(
            [partial[i * bs:(i + 1) * bs, i * bs:], partial[k * bs:(k + 1) * bs, k * bs:]], axis=1))
    packed = jnp.stack(rows)
    n = lax.axis_size(AXES)
    summed = sum_all(packed.reshape(n, -1)).reshape(packed.shape)
    lead = (nb // 2 - 1) * bs
    padded = jnp.pad(summed, ((0, 0), (0, 0), (lead, 0)))
    width = padded.shape[2]
    upper = []
    for r in range(nb):
        if r < nb // 2:
            start = lead - r * bs
            upper.append(padded[r, :, start:start + size])
        else:
            upper.append(padded[nb - 1 - r, :, width - size:])
    half = jnp.concatenate(upper, axis=0)
    blk = lax.broadcasted_iota(jnp.int32, (size, size), 0) // bs
    blk_t = lax.broadcasted_iota(jnp.int32, (size, size), 1) // bs
    return jnp.where(blk <= blk_t, half, half.T) * scale


def local(sky_cube, beam_blocks, pattern, start_modes):
    chans = sky_cube.shape[0]
    pix_group = sky_cube.shape[1]
    block_count = pix_group // BLK
    blocks = sky_cube.reshape(chans, block_count, BLK)
    n_chan = lax.axis_size("chan")
    chunks = smooth(blocks, beam_blocks, pattern, n_chan)
    by_pixel = lax.all_to_all(chunks, "chan", 0, 0, tiled=True)
    by_pixel = by_pixel.reshape((n_chan * chans,) + by_pixel.shape[2:])
    all_pixels = pix_group * lax.axis_size("pix")
    basis = start_modes
    partial_value = lax.dot_general(
        by_pixel, by_pixel, (((1, 2), (1, 2)), ((), ())), preferred_element_type=jnp.float32)
    gram = symmetric_sum(partial_value, n_chan, 1.0 / all_pixels)
    for sweep in range(ITERS):
        images = jnp.dot(gram, basis, precision=lax.Precision.HIGHEST)
        basis = orthonormal(images)
    modes_low = basis.astype(jnp.bfloat16)
    coeffs = jnp.einsum("cm,cbi->mbi", modes_low, by_pixel, preferred_element_type=jnp.float32).astype(jnp.bfloat16)
    spread = jnp.broadcast_to(coeffs[None], (n_chan,) + coeffs.shape)
    gathered = lax.all_to_all(spread, "chan", 0, 0, tiled=False)
    me = lax.axis_index("chan")
    my_modes = lax.dynamic_slice_in_dim(modes_low, me * chans, chans, axis=0)
    removed = jnp.einsum("cm,jmbi->cjbi", my_modes, gathered, preferred_element_type=jnp.float32)
    cleaned = (chunks.transpose(1, 0, 2, 3).astype(jnp.float32) - removed).astype(jnp.bfloat16)
    cleaned = cleaned.reshape(chans, pix_group)
    return (cleaned, basis)


def solution(mesh):
    return jax.shard_map(
        local,
        mesh=mesh,
        in_specs=(P("chan", "pix"), P("chan", None, None, None), P("chan", None, None), P()),
        out_specs=(P("chan", "pix"), P()),
        check_vma=False,
    )
```

```python
import jax
import jax.numpy as jnp
from jax import lax
from jax.sharding import PartitionSpec as P
import functools
from jax.experimental import pallas as pl

BLK = 128
ITERS = 3
AXES = ("chan", "pix")
CT = 8

def smooth_kernel(pat_ref, sky_ref, beam_ref, out_ref):
    taps = beam_ref.shape[1]
    nblk = sky_ref.shape[1]
    lane = lax.broadcasted_iota(jnp.int32, (nblk, nblk), 1).astype(jnp.float32)
    row = lax.broadcasted_iota(jnp.int32, (nblk, nblk), 0)
    eye = jnp.where(row == lax.broadcasted_iota(jnp.int32, (nblk, nblk), 1), 1.0, 0.0).astype(jnp.bfloat16)
    one = jnp.ones((nblk, nblk), jnp.float32)
    zero = jnp.zeros((nblk, nblk), jnp.float32)
    ct = sky_ref.shape[0]
    pat = pat_ref[...].reshape(taps * ct, nblk).astype(jnp.float32).astype(jnp.bfloat16)
    pat = lax.dot_general(eye, pat, (((1,), (1,)), ((), ())), preferred_element_type=jnp.float32)
    for c in range(ct):
        sel = jnp.concatenate(
            [jnp.where(pat[:, k * ct + c:k * ct + c + 1] == lane, one, zero).astype(jnp.bfloat16)
             for k in range(taps)], axis=0)
        src = jnp.dot(sel, sky_ref[c], preferred_element_type=jnp.float32).astype(jnp.bfloat16)
        lhs = jnp.concatenate([src[k * nblk:(k + 1) * nblk] for k in range(taps)], axis=1)
        rhs = jnp.concatenate([beam_ref[c, k] for k in range(taps)], axis=1)
        out = lax.dot_general(lhs, rhs, (((1,), (1,)), ((), ())), preferred_element_type=jnp.float32)
        out_ref[:, c] = out.astype(out_ref.dtype).reshape(out_ref.shape[0], out_ref.shape[2], out_ref.shape[3])

def smooth(sky3, beam, pattern, parts):
    chans, nblk, blk = sky3.shape
    taps = beam.shape[1]
    pat_t = jnp.transpose(pattern, (2, 0, 1))
    return pl.pallas_call(
        smooth_kernel,
        out_shape=jax.ShapeDtypeStruct((parts, chans, nblk // parts, blk), jnp.bfloat16),
        grid=(chans // CT,),
        in_specs=[pl.BlockSpec((taps, CT, nblk), lambda i: (0, i, 0)),
                  pl.BlockSpec((CT, nblk, blk), lambda i: (i, 0, 0)),
                  pl.BlockSpec((CT, taps, blk, blk), lambda i: (i, 0, 0, 0))],
        out_specs=pl.BlockSpec((parts, CT, nblk // parts, blk), lambda i: (0, i, 0, 0)),
    )(pat_t, sky3, beam)


HI = lax.Precision.HIGHEST

def sweep_kernel(g_ref, b_ref, o_ref, *, iters):
    g = g_ref[...]
    bt = b_ref[...]
    m = bt.shape[0]
    rows = lax.broadcasted_iota(jnp.int32, (m, m), 0)
    cols = lax.broadcasted_iota(jnp.int32, (m, m), 1)
    for _ in range(iters):
        it = jnp.dot(bt, g, precision=HI, preferred_element_type=jnp.float32)
        a = lax.dot_general(it, it, (((1,), (1,)), ((), ())), precision=HI,
                            preferred_element_type=jnp.float32)
        low = jnp.zeros((m, m), jnp.float32)
        for j in range(m):
            d = jnp.sqrt(a[j:j + 1, j:j + 1])
            col = jnp.where(rows[:, j:j + 1] >= j, a[:, j:j + 1] / d, 0.0)
            row = jnp.where(cols[j:j + 1, :] >= j, a[j:j + 1, :] / d, 0.0)
            low = jnp.where(cols == j, col, low)
            a = a - col * row
        bad = jnp.isnan(jnp.sum(low, keepdims=True))
        low = jnp.where(bad, jnp.nan, low)
        rest = jnp.where(rows == cols, 1.0, 0.0).astype(jnp.float32)
        inv = jnp.zeros((m, m), jnp.float32)
        for i in range(m):
            r = rest[i:i + 1, :] / low[i:i + 1, i:i + 1]
            inv = jnp.where(rows == i, r, inv)
            rest = rest - low[:, i:i + 1] * r
        bt = jnp.dot(inv, it, precision=HI, preferred_element_type=jnp.float32)
    o_ref[...] = bt

def sweeps(gram, basis, iters):
    bt = basis.T
    out = pl.pallas_call(
        functools.partial(sweep_kernel, iters=iters),
        out_shape=jax.ShapeDtypeStruct(bt.shape, jnp.float32),
    )(gram, bt)
    return out.T


def sum_all(pieces):
    n = pieces.shape[0]
    got = lax.all_to_all(pieces, AXES, 0, 0, tiled=False)
    mine = jnp.sum(got, axis=0)
    spread = jnp.broadcast_to(mine[None], (n,) + mine.shape)
    return lax.all_to_all(spread, AXES, 0, 0, tiled=False)


def symmetric_sum(partial, nb, scale):
    size = partial.shape[0]
    bs = size // nb
    rows = []
    for i in range(nb // 2):
        k = nb - 1 - i
        rows.append(jnp.concatenate(
            [partial[i * bs:(i + 1) * bs, i * bs:], partial[k * bs:(k + 1) * bs, k * bs:]], axis=1))
    packed = jnp.stack(rows)
    n = lax.axis_size(AXES)
    summed = sum_all(packed.reshape(n, -1)).reshape(packed.shape)
    lead = (nb // 2 - 1) * bs
    padded = jnp.pad(summed, ((0, 0), (0, 0), (lead, 0)))
    width = padded.shape[2]
    upper = []
    for r in range(nb):
        if r < nb // 2:
            start = lead - r * bs
            upper.append(padded[r, :, start:start + size])
        else:
            upper.append(padded[nb - 1 - r, :, width - size:])
    half = jnp.concatenate(upper, axis=0)
    blk = lax.broadcasted_iota(jnp.int32, (size, size), 0) // bs
    blk_t = lax.broadcasted_iota(jnp.int32, (size, size), 1) // bs
    return jnp.where(blk <= blk_t, half, half.T) * scale


def local(sky_cube, beam_blocks, pattern, start_modes):
    chans = sky_cube.shape[0]
    pix_group = sky_cube.shape[1]
    block_count = pix_group // BLK
    blocks = sky_cube.reshape(chans, block_count, BLK)
    n_chan = lax.axis_size("chan")
    chunks = smooth(blocks, beam_blocks, pattern, n_chan)
    by_pixel = lax.all_to_all(chunks, "chan", 0, 0, tiled=True)
    by_pixel = by_pixel.reshape((n_chan * chans,) + by_pixel.shape[2:])
    all_pixels = pix_group * lax.axis_size("pix")
    basis = start_modes
    partial_value = lax.dot_general(
        by_pixel, by_pixel, (((1, 2), (1, 2)), ((), ())), preferred_element_type=jnp.float32)
    gram = symmetric_sum(partial_value, n_chan, 1.0 / all_pixels)
    basis = sweeps(gram, basis, ITERS)
    modes_low = basis.astype(jnp.bfloat16)
    coeffs = jnp.einsum("cm,cbi->mbi", modes_low, by_pixel, preferred_element_type=jnp.float32).astype(jnp.bfloat16)
    spread = jnp.broadcast_to(coeffs[None], (n_chan,) + coeffs.shape)
    gathered = lax.all_to_all(spread, "chan", 0, 0, tiled=False)
    me = lax.axis_index("chan")
    my_modes = lax.dynamic_slice_in_dim(modes_low, me * chans, chans, axis=0)
    removed = jnp.einsum("cm,jmbi->cjbi", my_modes, gathered, preferred_element_type=jnp.float32)
    cleaned = (chunks.transpose(1, 0, 2, 3).astype(jnp.float32) - removed).astype(jnp.bfloat16)
    cleaned = cleaned.reshape(chans, pix_group)
    return (cleaned, basis)


def solution(mesh):
    return jax.shard_map(
        local,
        mesh=mesh,
        in_specs=(P("chan", "pix"), P("chan", None, None, None), P("chan", None, None), P()),
        out_specs=(P("chan", "pix"), P()),
        check_vma=False,
    )
```

```python
import jax
import jax.numpy as jnp
from jax import lax
from jax.sharding import PartitionSpec as P
import functools
from jax.experimental import pallas as pl

BLK = 128
ITERS = 3
AXES = ("chan", "pix")
CT = 8

def smooth_kernel(pat_ref, sky_ref, beam_ref, out_ref):
    taps = beam_ref.shape[1]
    nblk = sky_ref.shape[1]
    lane = lax.broadcasted_iota(jnp.int32, (nblk, nblk), 1).astype(jnp.float32)
    row = lax.broadcasted_iota(jnp.int32, (nblk, nblk), 0)
    eye = jnp.where(row == lax.broadcasted_iota(jnp.int32, (nblk, nblk), 1), 1.0, 0.0).astype(jnp.bfloat16)
    one = jnp.ones((nblk, nblk), jnp.float32)
    zero = jnp.zeros((nblk, nblk), jnp.float32)
    ct = sky_ref.shape[0]
    pat = pat_ref[...].reshape(taps * ct, nblk).astype(jnp.float32).astype(jnp.bfloat16)
    pat = lax.dot_general(eye, pat, (((1,), (1,)), ((), ())), preferred_element_type=jnp.float32)
    for c in range(ct):
        sel = jnp.concatenate(
            [jnp.where(pat[:, k * ct + c:k * ct + c + 1] == lane, one, zero).astype(jnp.bfloat16)
             for k in range(taps)], axis=0)
        src = jnp.dot(sel, sky_ref[c], preferred_element_type=jnp.float32).astype(jnp.bfloat16)
        lhs = jnp.concatenate([src[k * nblk:(k + 1) * nblk] for k in range(taps)], axis=1)
        rhs = jnp.concatenate([beam_ref[c, k] for k in range(taps)], axis=1)
        out = lax.dot_general(lhs, rhs, (((1,), (1,)), ((), ())), preferred_element_type=jnp.float32)
        out_ref[:, c] = out.astype(out_ref.dtype).reshape(out_ref.shape[0], out_ref.shape[2], out_ref.shape[3])

def smooth(sky3, beam, pattern, parts):
    chans, nblk, blk = sky3.shape
    taps = beam.shape[1]
    pat_t = jnp.transpose(pattern, (2, 0, 1))
    return pl.pallas_call(
        smooth_kernel,
        out_shape=jax.ShapeDtypeStruct((parts, chans, nblk // parts, blk), jnp.bfloat16),
        grid=(chans // CT,),
        in_specs=[pl.BlockSpec((taps, CT, nblk), lambda i: (0, i, 0)),
                  pl.BlockSpec((CT, nblk, blk), lambda i: (i, 0, 0)),
                  pl.BlockSpec((CT, taps, blk, blk), lambda i: (i, 0, 0, 0))],
        out_specs=pl.BlockSpec((parts, CT, nblk // parts, blk), lambda i: (0, i, 0, 0)),
    )(pat_t, sky3, beam)


HI = lax.Precision.HIGHEST

def build_gram(x, nb, bs, scale):
    n, w = x.shape
    pairs = nb // 2
    per = n // pairs
    span = (nb + 1) * bs
    q = w // span
    size = nb * bs
    mats = []
    for i in range(pairs):
        xi = x[i * per:(i + 1) * per]
        mats.append(jnp.concatenate([xi[:, h * span:(h + 1) * span] for h in range(q)], axis=0))
    rows = []
    for r in range(nb):
        if r < pairs:
            data = mats[r][:, :(nb - r) * bs]
            if r:
                data = jnp.concatenate([jnp.zeros((bs, r * bs), jnp.float32), data], axis=1)
            rows.append(data)
        else:
            rows.append(mats[nb - 1 - r][:, span - size:])
    half = jnp.concatenate(rows, axis=0)
    blk = lax.broadcasted_iota(jnp.int32, (size, size), 0) // bs
    blk_t = lax.broadcasted_iota(jnp.int32, (size, size), 1) // bs
    return jnp.where(blk <= blk_t, half, half.T) * scale


def sweep_kernel(g_ref, b_ref, o_ref, *, iters, nb, bs, scale):
    g = build_gram(g_ref[...], nb, bs, scale)
    bt = b_ref[...]
    m = bt.shape[0]
    rows = lax.broadcasted_iota(jnp.int32, (m, m), 0)
    cols = lax.broadcasted_iota(jnp.int32, (m, m), 1)
    for _ in range(iters):
        it = jnp.dot(bt, g, precision=HI, preferred_element_type=jnp.float32)
        a = lax.dot_general(it, it, (((1,), (1,)), ((), ())), precision=HI,
                            preferred_element_type=jnp.float32)
        low = jnp.zeros((m, m), jnp.float32)
        for j in range(m):
            d = jnp.sqrt(a[j:j + 1, j:j + 1])
            col = jnp.where(rows[:, j:j + 1] >= j, a[:, j:j + 1] / d, 0.0)
            row = jnp.where(cols[j:j + 1, :] >= j, a[j:j + 1, :] / d, 0.0)
            low = jnp.where(cols == j, col, low)
            a = a - col * row
        bad = jnp.isnan(jnp.sum(low, keepdims=True))
        low = jnp.where(bad, jnp.nan, low)
        rest = jnp.where(rows == cols, 1.0, 0.0).astype(jnp.float32)
        inv = jnp.zeros((m, m), jnp.float32)
        for i in range(m):
            r = rest[i:i + 1, :] / low[i:i + 1, i:i + 1]
            inv = jnp.where(rows == i, r, inv)
            rest = rest - low[:, i:i + 1] * r
        bt = jnp.dot(inv, it, precision=HI, preferred_element_type=jnp.float32)
    o_ref[...] = bt

def sweeps(packed, basis, iters, nb, bs, scale):
    bt = basis.T
    out = pl.pallas_call(
        functools.partial(sweep_kernel, iters=iters, nb=nb, bs=bs, scale=scale),
        out_shape=jax.ShapeDtypeStruct(bt.shape, jnp.float32),
    )(packed, bt)
    return out.T


def sum_all(pieces):
    n = pieces.shape[0]
    got = lax.all_to_all(pieces, AXES, 0, 0, tiled=False)
    mine = jnp.sum(got, axis=0)
    spread = jnp.broadcast_to(mine[None], (n,) + mine.shape)
    return lax.all_to_all(spread, AXES, 0, 0, tiled=False)


def pack_gram(partial, nb, n):
    size = partial.shape[0]
    bs = size // nb
    pairs = nb // 2
    q = bs * pairs // n
    out = []
    for i in range(pairs):
        k = nb - 1 - i
        m = jnp.concatenate(
            [partial[i * bs:(i + 1) * bs, i * bs:], partial[k * bs:(k + 1) * bs, k * bs:]], axis=1)
        rows = bs // q
        out.append(jnp.concatenate([m[h * rows:(h + 1) * rows] for h in range(q)], axis=1))
    return jnp.concatenate(out, axis=0)


def local(sky_cube, beam_blocks, pattern, start_modes):
    chans = sky_cube.shape[0]
    pix_group = sky_cube.shape[1]
    block_count = pix_group // BLK
    blocks = sky_cube.reshape(chans, block_count, BLK)
    n_chan = lax.axis_size("chan")
    chunks = smooth(blocks, beam_blocks, pattern, n_chan)
    by_pixel = lax.all_to_all(chunks, "chan", 0, 0, tiled=True)
    by_pixel = by_pixel.reshape((n_chan * chans,) + by_pixel.shape[2:])
    all_pixels = pix_group * lax.axis_size("pix")
    basis = start_modes
    partial_value = lax.dot_general(
        by_pixel, by_pixel, (((1, 2), (1, 2)), ((), ())), preferred_element_type=jnp.float32)
    nb = 4
    n_dev = lax.axis_size(AXES)
    packed = sum_all(pack_gram(partial_value, nb, n_dev))
    packed = packed.reshape(n_dev, -1)
    basis = sweeps(packed, basis, ITERS, nb, partial_value.shape[0] // nb, 1.0 / all_pixels)
    modes_low = basis.astype(jnp.bfloat16)
    coeffs = jnp.einsum("cm,cbi->mbi", modes_low, by_pixel, preferred_element_type=jnp.float32).astype(jnp.bfloat16)
    spread = jnp.broadcast_to(coeffs[None], (n_chan,) + coeffs.shape)
    gathered = lax.all_to_all(spread, "chan", 0, 0, tiled=False)
    me = lax.axis_index("chan")
    my_modes = lax.dynamic_slice_in_dim(modes_low, me * chans, chans, axis=0)
    removed = jnp.einsum("cm,jmbi->cjbi", my_modes, gathered, preferred_element_type=jnp.float32)
    cleaned = (chunks.transpose(1, 0, 2, 3).astype(jnp.float32) - removed).astype(jnp.bfloat16)
    cleaned = cleaned.reshape(chans, pix_group)
    return (cleaned, basis)


def solution(mesh):
    return jax.shard_map(
        local,
        mesh=mesh,
        in_specs=(P("chan", "pix"), P("chan", None, None, None), P("chan", None, None), P()),
        out_specs=(P("chan", "pix"), P()),
        check_vma=False,
    )
```

```python
import jax
import jax.numpy as jnp
from jax import lax
from jax.sharding import PartitionSpec as P
import functools
from jax.experimental import pallas as pl

BLK = 128
ITERS = 3
AXES = ("chan", "pix")
CT = 8

def smooth_kernel(pat_ref, sky_ref, beam_ref, out_ref):
    taps = beam_ref.shape[1]
    nblk = sky_ref.shape[1]
    lane = lax.broadcasted_iota(jnp.int32, (nblk, nblk), 1).astype(jnp.float32)
    row = lax.broadcasted_iota(jnp.int32, (nblk, nblk), 0)
    eye = jnp.where(row == lax.broadcasted_iota(jnp.int32, (nblk, nblk), 1), 1.0, 0.0).astype(jnp.bfloat16)
    one = jnp.ones((nblk, nblk), jnp.float32)
    zero = jnp.zeros((nblk, nblk), jnp.float32)
    ct = sky_ref.shape[0]
    pat = pat_ref[...].reshape(taps * ct, nblk).astype(jnp.float32).astype(jnp.bfloat16)
    pat = lax.dot_general(eye, pat, (((1,), (1,)), ((), ())), preferred_element_type=jnp.float32)
    for c in range(ct):
        sel = jnp.concatenate(
            [jnp.where(pat[:, k * ct + c:k * ct + c + 1] == lane, one, zero).astype(jnp.bfloat16)
             for k in range(taps)], axis=0)
        src = jnp.dot(sel, sky_ref[c], preferred_element_type=jnp.float32).astype(jnp.bfloat16)
        lhs = jnp.concatenate([src[k * nblk:(k + 1) * nblk] for k in range(taps)], axis=1)
        rhs = jnp.concatenate([beam_ref[c, k] for k in range(taps)], axis=1)
        out = lax.dot_general(lhs, rhs, (((1,), (1,)), ((), ())), preferred_element_type=jnp.float32)
        out_ref[:, c] = out.astype(out_ref.dtype).reshape(out_ref.shape[0], out_ref.shape[2], out_ref.shape[3])

def smooth(sky3, beam, pat_t, parts, first, steps):
    chans, nblk, blk = sky3.shape
    taps = beam.shape[1]
    return pl.pallas_call(
        smooth_kernel,
        out_shape=jax.ShapeDtypeStruct((parts, steps * CT, nblk // parts, blk), jnp.bfloat16),
        grid=(steps,),
        in_specs=[pl.BlockSpec((taps, CT, nblk), lambda i: (0, i + first, 0)),
                  pl.BlockSpec((CT, nblk, blk), lambda i: (i + first, 0, 0)),
                  pl.BlockSpec((CT, taps, blk, blk), lambda i: (i + first, 0, 0, 0))],
        out_specs=pl.BlockSpec((parts, CT, nblk // parts, blk), lambda i: (0, i, 0, 0)),
    )(pat_t, sky3, beam)


HI = lax.Precision.HIGHEST

def build_gram(x, nb, bs, scale):
    n, w = x.shape
    pairs = nb // 2
    per = n // pairs
    span = (nb + 1) * bs
    q = w // span
    size = nb * bs
    mats = []
    for i in range(pairs):
        xi = x[i * per:(i + 1) * per]
        mats.append(jnp.concatenate([xi[:, h * span:(h + 1) * span] for h in range(q)], axis=0))
    rows = []
    for r in range(nb):
        if r < pairs:
            data = mats[r][:, :(nb - r) * bs]
            if r:
                data = jnp.concatenate([jnp.zeros((bs, r * bs), jnp.float32), data], axis=1)
            rows.append(data)
        else:
            rows.append(mats[nb - 1 - r][:, span - size:])
    half = jnp.concatenate(rows, axis=0)
    blk = lax.broadcasted_iota(jnp.int32, (size, size), 0) // bs
    blk_t = lax.broadcasted_iota(jnp.int32, (size, size), 1) // bs
    return jnp.where(blk <= blk_t, half, half.T) * scale


def sweep_kernel(g_ref, b_ref, o_ref, *, iters, nb, bs, scale):
    g = build_gram(g_ref[...], nb, bs, scale)
    bt = b_ref[...]
    m = bt.shape[0]
    rows = lax.broadcasted_iota(jnp.int32, (m, m), 0)
    cols = lax.broadcasted_iota(jnp.int32, (m, m), 1)
    for _ in range(iters):
        it = jnp.dot(bt, g, precision=HI, preferred_element_type=jnp.float32)
        a = lax.dot_general(it, it, (((1,), (1,)), ((), ())), precision=HI,
                            preferred_element_type=jnp.float32)
        low = jnp.zeros((m, m), jnp.float32)
        for j in range(m):
            d = jnp.sqrt(a[j:j + 1, j:j + 1])
            col = jnp.where(rows[:, j:j + 1] >= j, a[:, j:j + 1] / d, 0.0)
            row = jnp.where(cols[j:j + 1, :] >= j, a[j:j + 1, :] / d, 0.0)
            low = jnp.where(cols == j, col, low)
            a = a - col * row
        bad = jnp.isnan(jnp.sum(low, keepdims=True))
        low = jnp.where(bad, jnp.nan, low)
        rest = jnp.where(rows == cols, 1.0, 0.0).astype(jnp.float32)
        inv = jnp.zeros((m, m), jnp.float32)
        for i in range(m):
            r = rest[i:i + 1, :] / low[i:i + 1, i:i + 1]
            inv = jnp.where(rows == i, r, inv)
            rest = rest - low[:, i:i + 1] * r
        bt = jnp.dot(inv, it, precision=HI, preferred_element_type=jnp.float32)
    o_ref[...] = bt

def sweeps(packed, basis, iters, nb, bs, scale):
    bt = basis.T
    out = pl.pallas_call(
        functools.partial(sweep_kernel, iters=iters, nb=nb, bs=bs, scale=scale),
        out_shape=jax.ShapeDtypeStruct(bt.shape, jnp.float32),
    )(packed, bt)
    return out.T


def sum_all(pieces):
    n = pieces.shape[0]
    got = lax.all_to_all(pieces, AXES, 0, 0, tiled=False)
    mine = jnp.sum(got, axis=0)
    spread = jnp.broadcast_to(mine[None], (n,) + mine.shape)
    return lax.all_to_all(spread, AXES, 0, 0, tiled=False)


def pack_gram(partial, nb, n):
    size = partial.shape[0]
    bs = size // nb
    pairs = nb // 2
    q = bs * pairs // n
    out = []
    for i in range(pairs):
        k = nb - 1 - i
        m = jnp.concatenate(
            [partial[i * bs:(i + 1) * bs, i * bs:], partial[k * bs:(k + 1) * bs, k * bs:]], axis=1)
        rows = bs // q
        out.append(jnp.concatenate([m[h * rows:(h + 1) * rows] for h in range(q)], axis=1))
    return jnp.concatenate(out, axis=0)


def local(sky_cube, beam_blocks, pattern, start_modes):
    chans = sky_cube.shape[0]
    pix_group = sky_cube.shape[1]
    block_count = pix_group // BLK
    blocks = sky_cube.reshape(chans, block_count, BLK)
    n_chan = lax.axis_size("chan")
    halves = []
    got = []
    pat_t = jnp.transpose(pattern, (2, 0, 1))
    steps = chans // CT // 2
    for part in range(2):
        c_part = smooth(blocks, beam_blocks, pat_t, n_chan, part * steps, steps)
        halves.append(c_part)
        got.append(lax.all_to_all(c_part, "chan", 0, 0, tiled=True))
    chunks = jnp.concatenate(halves, axis=1)
    by_pixel = jnp.concatenate(got, axis=1)
    by_pixel = by_pixel.reshape((n_chan * chans,) + by_pixel.shape[2:])
    all_pixels = pix_group * lax.axis_size("pix")
    basis = start_modes
    partial_value = lax.dot_general(
        by_pixel, by_pixel, (((1, 2), (1, 2)), ((), ())), preferred_element_type=jnp.float32)
    nb = 4
    n_dev = lax.axis_size(AXES)
    packed = sum_all(pack_gram(partial_value, nb, n_dev))
    packed = packed.reshape(n_dev, -1)
    basis = sweeps(packed, basis, ITERS, nb, partial_value.shape[0] // nb, 1.0 / all_pixels)
    modes_low = basis.astype(jnp.bfloat16)
    coeffs = jnp.einsum("cm,cbi->mbi", modes_low, by_pixel, preferred_element_type=jnp.float32).astype(jnp.bfloat16)
    spread = jnp.broadcast_to(coeffs[None], (n_chan,) + coeffs.shape)
    gathered = lax.all_to_all(spread, "chan", 0, 0, tiled=False)
    me = lax.axis_index("chan")
    my_modes = lax.dynamic_slice_in_dim(modes_low, me * chans, chans, axis=0)
    removed = jnp.einsum("cm,jmbi->cjbi", my_modes, gathered, preferred_element_type=jnp.float32)
    cleaned = (chunks.transpose(1, 0, 2, 3).astype(jnp.float32) - removed).astype(jnp.bfloat16)
    cleaned = cleaned.reshape(chans, pix_group)
    return (cleaned, basis)


def solution(mesh):
    return jax.shard_map(
        local,
        mesh=mesh,
        in_specs=(P("chan", "pix"), P("chan", None, None, None), P("chan", None, None), P()),
        out_specs=(P("chan", "pix"), P()),
        check_vma=False,
    )
```

```python
import jax
import jax.numpy as jnp
from jax import lax
from jax.sharding import PartitionSpec as P
import functools
from jax.experimental import pallas as pl

BLK = 128
ITERS = 3
AXES = ("chan", "pix")
CT = 8

def smooth_kernel(pat_ref, sky_ref, beam_ref, out_ref):
    taps = beam_ref.shape[1]
    nblk = sky_ref.shape[1]
    ct = sky_ref.shape[0]
    sub = lax.broadcasted_iota(jnp.int32, (nblk, nblk), 0)
    one = jnp.ones((nblk, nblk), jnp.float32)
    zero = jnp.zeros((nblk, nblk), jnp.float32)
    pat = pat_ref[...]
    for c in range(ct):
        selt = jnp.concatenate(
            [jnp.where(pat[k, c:c + 1, :] == sub, one, zero).astype(jnp.bfloat16) for k in range(taps)], axis=1)
        srct = lax.dot_general(sky_ref[c], selt, (((0,), (0,)), ((), ())),
                               preferred_element_type=jnp.float32).astype(jnp.bfloat16)
        stacked = jnp.concatenate([srct[:, k * nblk:(k + 1) * nblk] for k in range(taps)], axis=0)
        rhs = jnp.concatenate([beam_ref[c, k] for k in range(taps)], axis=1)
        outt = jnp.dot(rhs, stacked, preferred_element_type=jnp.float32)
        out = outt.T
        out_ref[:, c] = out.astype(out_ref.dtype).reshape(out_ref.shape[0], out_ref.shape[2], out_ref.shape[3])

def smooth(sky3, beam, pat_t, parts, first, steps):
    chans, nblk, blk = sky3.shape
    taps = beam.shape[1]
    return pl.pallas_call(
        smooth_kernel,
        out_shape=jax.ShapeDtypeStruct((parts, steps * CT, nblk // parts, blk), jnp.bfloat16),
        grid=(steps,),
        in_specs=[pl.BlockSpec((taps, CT, nblk), lambda i: (0, i + first, 0)),
                  pl.BlockSpec((CT, nblk, blk), lambda i: (i + first, 0, 0)),
                  pl.BlockSpec((CT, taps, blk, blk), lambda i: (i + first, 0, 0, 0))],
        out_specs=pl.BlockSpec((parts, CT, nblk // parts, blk), lambda i: (0, i, 0, 0)),
    )(pat_t, sky3, beam)


HI = lax.Precision.HIGHEST

def build_gram(x, nb, bs, scale):
    n, w = x.shape
    pairs = nb // 2
    per = n // pairs
    span = (nb + 1) * bs
    q = w // span
    size = nb * bs
    mats = []
    for i in range(pairs):
        xi = x[i * per:(i + 1) * per]
        mats.append(jnp.concatenate([xi[:, h * span:(h + 1) * span] for h in range(q)], axis=0))
    rows = []
    for r in range(nb):
        if r < pairs:
            data = mats[r][:, :(nb - r) * bs]
            if r:
                data = jnp.concatenate([jnp.zeros((bs, r * bs), jnp.float32), data], axis=1)
            rows.append(data)
        else:
            rows.append(mats[nb - 1 - r][:, span - size:])
    half = jnp.concatenate(rows, axis=0)
    blk = lax.broadcasted_iota(jnp.int32, (size, size), 0) // bs
    blk_t = lax.broadcasted_iota(jnp.int32, (size, size), 1) // bs
    return jnp.where(blk <= blk_t, half, half.T) * scale


def sweep_kernel(g_ref, b_ref, o_ref, *, iters, nb, bs, scale):
    g = build_gram(g_ref[...], nb, bs, scale)
    bt = b_ref[...]
    m = bt.shape[0]
    rows = lax.broadcasted_iota(jnp.int32, (m, m), 0)
    cols = lax.broadcasted_iota(jnp.int32, (m, m), 1)
    for _ in range(iters):
        it = jnp.dot(bt, g, precision=HI, preferred_element_type=jnp.float32)
        a = lax.dot_general(it, it, (((1,), (1,)), ((), ())), precision=HI,
                            preferred_element_type=jnp.float32)
        rest = jnp.where(rows == cols, 1.0, 0.0).astype(jnp.float32)
        inv = jnp.zeros((m, m), jnp.float32)
        for j in range(m):
            d = jnp.sqrt(a[j:j + 1, j:j + 1])
            col = jnp.where(rows[:, j:j + 1] >= j, a[:, j:j + 1] / d, 0.0)
            row = jnp.where(cols[j:j + 1, :] >= j, a[j:j + 1, :] / d, 0.0)
            a = a - col * row
            r = rest[j:j + 1, :] / d
            inv = jnp.where(rows == j, r, inv)
            rest = rest - col * r
        bad = jnp.isnan(jnp.sum(inv, keepdims=True))
        inv = jnp.where(bad, jnp.nan, inv)
        bt = jnp.dot(inv, it, precision=HI, preferred_element_type=jnp.float32)
    o_ref[...] = bt

def sweeps(packed, basis, iters, nb, bs, scale):
    bt = basis.T
    out = pl.pallas_call(
        functools.partial(sweep_kernel, iters=iters, nb=nb, bs=bs, scale=scale),
        out_shape=jax.ShapeDtypeStruct(bt.shape, jnp.float32),
    )(packed, bt)
    return out.T


def sum_all(pieces):
    n = pieces.shape[0]
    got = lax.all_to_all(pieces, AXES, 0, 0, tiled=False)
    mine = jnp.sum(got, axis=0)
    spread = jnp.broadcast_to(mine[None], (n,) + mine.shape)
    return lax.all_to_all(spread, AXES, 0, 0, tiled=False)


def pack_gram(partial, nb, n):
    size = partial.shape[0]
    bs = size // nb
    pairs = nb // 2
    q = bs * pairs // n
    out = []
    for i in range(pairs):
        k = nb - 1 - i
        m = jnp.concatenate(
            [partial[i * bs:(i + 1) * bs, i * bs:], partial[k * bs:(k + 1) * bs, k * bs:]], axis=1)
        rows = bs // q
        out.append(jnp.concatenate([m[h * rows:(h + 1) * rows] for h in range(q)], axis=1))
    return jnp.concatenate(out, axis=0)


def local(sky_cube, beam_blocks, pattern, start_modes):
    chans = sky_cube.shape[0]
    pix_group = sky_cube.shape[1]
    block_count = pix_group // BLK
    blocks = sky_cube.reshape(chans, block_count, BLK)
    n_chan = lax.axis_size("chan")
    halves = []
    got = []
    pat_t = jnp.transpose(pattern, (2, 0, 1))
    steps = chans // CT // 2
    for part in range(2):
        c_part = smooth(blocks, beam_blocks, pat_t, n_chan, part * steps, steps)
        halves.append(c_part)
        got.append(lax.all_to_all(c_part, "chan", 0, 0, tiled=True))
    chunks = jnp.concatenate(halves, axis=1)
    by_pixel = jnp.concatenate(got, axis=1)
    by_pixel = by_pixel.reshape((n_chan * chans,) + by_pixel.shape[2:])
    all_pixels = pix_group * lax.axis_size("pix")
    basis = start_modes
    partial_value = lax.dot_general(
        by_pixel, by_pixel, (((1, 2), (1, 2)), ((), ())), preferred_element_type=jnp.float32)
    nb = 4
    n_dev = lax.axis_size(AXES)
    packed = sum_all(pack_gram(partial_value, nb, n_dev))
    packed = packed.reshape(n_dev, -1)
    basis = sweeps(packed, basis, ITERS, nb, partial_value.shape[0] // nb, 1.0 / all_pixels)
    modes_low = basis.astype(jnp.bfloat16)
    coeffs = jnp.einsum("cm,cbi->mbi", modes_low, by_pixel, preferred_element_type=jnp.float32).astype(jnp.bfloat16)
    spread = jnp.broadcast_to(coeffs[None], (n_chan,) + coeffs.shape)
    gathered = lax.all_to_all(spread, "chan", 0, 0, tiled=False)
    me = lax.axis_index("chan")
    my_modes = lax.dynamic_slice_in_dim(modes_low, me * chans, chans, axis=0)
    removed = jnp.einsum("cm,jmbi->cjbi", my_modes, gathered, preferred_element_type=jnp.float32)
    cleaned = (chunks.transpose(1, 0, 2, 3).astype(jnp.float32) - removed).astype(jnp.bfloat16)
    cleaned = cleaned.reshape(chans, pix_group)
    return (cleaned, basis)


def solution(mesh):
    return jax.shard_map(
        local,
        mesh=mesh,
        in_specs=(P("chan", "pix"), P("chan", None, None, None), P("chan", None, None), P()),
        out_specs=(P("chan", "pix"), P()),
        check_vma=False,
    )
```

```python
import jax
import jax.numpy as jnp
from jax import lax
from jax.sharding import PartitionSpec as P
import functools
from jax.experimental import pallas as pl

BLK = 128
ITERS = 3
AXES = ("chan", "pix")
CT = 8

def smooth_kernel(pat_ref, sky_ref, beam_ref, out_ref):
    taps = beam_ref.shape[1]
    nblk = sky_ref.shape[1]
    ct = sky_ref.shape[0]
    sub = lax.broadcasted_iota(jnp.int32, (nblk, nblk), 0)
    one = jnp.ones((nblk, nblk), jnp.float32)
    zero = jnp.zeros((nblk, nblk), jnp.float32)
    pat = pat_ref[...]
    for c in range(ct):
        selt = jnp.concatenate(
            [jnp.where(pat[k, c:c + 1, :] == sub, one, zero).astype(jnp.bfloat16) for k in range(taps)], axis=1)
        srct = lax.dot_general(sky_ref[c], selt, (((0,), (0,)), ((), ())),
                               preferred_element_type=jnp.float32).astype(jnp.bfloat16)
        stacked = jnp.concatenate([srct[:, k * nblk:(k + 1) * nblk] for k in range(taps)], axis=0)
        rhs = jnp.concatenate([beam_ref[c, k] for k in range(taps)], axis=1)
        outt = jnp.dot(rhs, stacked, preferred_element_type=jnp.float32)
        out = outt.T
        out_ref[:, c] = out.astype(out_ref.dtype).reshape(out_ref.shape[0], out_ref.shape[2], out_ref.shape[3])

def smooth(sky3, beam, pat_t, parts, first, steps):
    chans, nblk, blk = sky3.shape
    taps = beam.shape[1]
    return pl.pallas_call(
        smooth_kernel,
        out_shape=jax.ShapeDtypeStruct((parts, steps * CT, nblk // parts, blk), jnp.bfloat16),
        grid=(steps,),
        in_specs=[pl.BlockSpec((taps, CT, nblk), lambda i: (0, i + first, 0)),
                  pl.BlockSpec((CT, nblk, blk), lambda i: (i + first, 0, 0)),
                  pl.BlockSpec((CT, taps, blk, blk), lambda i: (i + first, 0, 0, 0))],
        out_specs=pl.BlockSpec((parts, CT, nblk // parts, blk), lambda i: (0, i, 0, 0)),
    )(pat_t, sky3, beam)


HI = lax.Precision.HIGHEST

def build_gram(x, nb, bs, scale):
    n, w = x.shape
    pairs = nb // 2
    per = n // pairs
    span = (nb + 1) * bs
    q = w // span
    size = nb * bs
    mats = []
    for i in range(pairs):
        xi = x[i * per:(i + 1) * per]
        mats.append(jnp.concatenate([xi[:, h * span:(h + 1) * span] for h in range(q)], axis=0))
    rows = []
    for r in range(nb):
        if r < pairs:
            data = mats[r][:, :(nb - r) * bs]
            if r:
                data = jnp.concatenate([jnp.zeros((bs, r * bs), jnp.float32), data], axis=1)
            rows.append(data)
        else:
            rows.append(mats[nb - 1 - r][:, span - size:])
    half = jnp.concatenate(rows, axis=0)
    blk = lax.broadcasted_iota(jnp.int32, (size, size), 0) // bs
    blk_t = lax.broadcasted_iota(jnp.int32, (size, size), 1) // bs
    return jnp.where(blk <= blk_t, half, half.T) * scale


def sweep_kernel(g_ref, b_ref, o_ref, *, iters, nb, bs, scale):
    g = build_gram(g_ref[...], nb, bs, scale)
    bt = b_ref[...]
    m = bt.shape[0]
    rows = lax.broadcasted_iota(jnp.int32, (m, m), 0)
    cols = lax.broadcasted_iota(jnp.int32, (m, m), 1)
    for _ in range(iters):
        it = jnp.dot(bt, g, precision=HI, preferred_element_type=jnp.float32)
        a = lax.dot_general(it, it, (((1,), (1,)), ((), ())), precision=HI,
                            preferred_element_type=jnp.float32)
        rest = jnp.where(rows == cols, 1.0, 0.0).astype(jnp.float32)
        inv = jnp.zeros((m, m), jnp.float32)
        for j in range(m):
            d = jnp.sqrt(a[j:j + 1, j:j + 1])
            col = jnp.where(rows[:, j:j + 1] >= j, a[:, j:j + 1] / d, 0.0)
            row = jnp.where(cols[j:j + 1, :] >= j, a[j:j + 1, :] / d, 0.0)
            a = a - col * row
            r = rest[j:j + 1, :] / d
            inv = jnp.where(rows == j, r, inv)
            rest = rest - col * r
        bad = jnp.isnan(jnp.sum(inv, keepdims=True))
        inv = jnp.where(bad, jnp.nan, inv)
        bt = jnp.dot(inv, it, precision=HI, preferred_element_type=jnp.float32)
    o_ref[...] = bt

def sweeps(packed, basis, iters, nb, bs, scale):
    bt = basis.T
    out = pl.pallas_call(
        functools.partial(sweep_kernel, iters=iters, nb=nb, bs=bs, scale=scale),
        out_shape=jax.ShapeDtypeStruct(bt.shape, jnp.float32),
    )(packed, bt)
    return out.T


def sum_all(pieces):
    n = pieces.shape[0]
    got = lax.all_to_all(pieces, AXES, 0, 0, tiled=False)
    mine = jnp.sum(got, axis=0)
    spread = jnp.broadcast_to(mine[None], (n,) + mine.shape)
    return lax.all_to_all(spread, AXES, 0, 0, tiled=False)


def pack_gram(partial, nb, n):
    size = partial.shape[0]
    bs = size // nb
    pairs = nb // 2
    q = bs * pairs // n
    out = []
    for i in range(pairs):
        k = nb - 1 - i
        m = jnp.concatenate(
            [partial[i * bs:(i + 1) * bs, i * bs:], partial[k * bs:(k + 1) * bs, k * bs:]], axis=1)
        rows = bs // q
        out.append(jnp.concatenate([m[h * rows:(h + 1) * rows] for h in range(q)], axis=1))
    return jnp.concatenate(out, axis=0)


def local(sky_cube, beam_blocks, pattern, start_modes):
    chans = sky_cube.shape[0]
    pix_group = sky_cube.shape[1]
    block_count = pix_group // BLK
    blocks = sky_cube.reshape(chans, block_count, BLK)
    n_chan = lax.axis_size("chan")
    halves = []
    got = []
    pat_t = jnp.transpose(pattern, (2, 0, 1))
    steps = chans // CT // 2
    for part in range(2):
        c_part = smooth(blocks, beam_blocks, pat_t, n_chan, part * steps, steps)
        halves.append(c_part)
        got.append(lax.all_to_all(c_part, "chan", 0, 0, tiled=True))
    chunks = jnp.concatenate(halves, axis=1)
    by_pixel = jnp.concatenate(got, axis=1)
    by_pixel = by_pixel.reshape((n_chan * chans,) + by_pixel.shape[2:])
    all_pixels = pix_group * lax.axis_size("pix")
    basis = start_modes
    partial_value = lax.dot_general(
        by_pixel, by_pixel, (((1, 2), (1, 2)), ((), ())), preferred_element_type=jnp.float32)
    nb = 4
    n_dev = lax.axis_size(AXES)
    packed = sum_all(pack_gram(partial_value, nb, n_dev))
    packed = packed.reshape(n_dev, -1)
    basis = sweeps(packed, basis, ITERS, nb, partial_value.shape[0] // nb, 1.0 / all_pixels)
    modes_low = basis.astype(jnp.bfloat16)
    coeffs = jnp.einsum("cm,cbi->mbi", modes_low, by_pixel, preferred_element_type=jnp.float32).astype(jnp.bfloat16)
    me = lax.axis_index("chan")
    my_modes = lax.dynamic_slice_in_dim(modes_low, me * chans, chans, axis=0)
    width = pix_group // n_chan
    cleaned = jnp.zeros((chans, pix_group), jnp.bfloat16)
    for shift in range(n_chan):
        if shift:
            part = lax.ppermute(coeffs, "chan", [(i, (i + shift) % n_chan) for i in range(n_chan)])
        else:
            part = coeffs
        src = (me - shift) % n_chan
        removed = jnp.einsum("cm,mbi->cbi", my_modes, part, preferred_element_type=jnp.float32)
        mine = lax.dynamic_index_in_dim(chunks, src, axis=0, keepdims=False)
        slab = (mine.astype(jnp.float32) - removed).astype(jnp.bfloat16).reshape(chans, width)
        cleaned = lax.dynamic_update_slice_in_dim(cleaned, slab, src * width, axis=1)
    return (cleaned, basis)


def solution(mesh):
    return jax.shard_map(
        local,
        mesh=mesh,
        in_specs=(P("chan", "pix"), P("chan", None, None, None), P("chan", None, None), P()),
        out_specs=(P("chan", "pix"), P()),
        check_vma=False,
    )
```

```python
import jax
import jax.numpy as jnp
from jax import lax
from jax.sharding import PartitionSpec as P
import functools
from jax.experimental import pallas as pl

BLK = 128
ITERS = 3
AXES = ("chan", "pix")
CT = 8

def smooth_kernel(pat_ref, sky_ref, beam_ref, out_ref):
    taps = beam_ref.shape[1]
    nblk = sky_ref.shape[1]
    ct = sky_ref.shape[0]
    sub = lax.broadcasted_iota(jnp.int32, (nblk, nblk), 0)
    one = jnp.ones((nblk, nblk), jnp.float32)
    zero = jnp.zeros((nblk, nblk), jnp.float32)
    pat = pat_ref[...]
    for c in range(ct):
        selt = jnp.concatenate(
            [jnp.where(pat[k, c:c + 1, :] == sub, one, zero).astype(jnp.bfloat16) for k in range(taps)], axis=1)
        srct = lax.dot_general(sky_ref[c], selt, (((0,), (0,)), ((), ())),
                               preferred_element_type=jnp.float32).astype(jnp.bfloat16)
        stacked = jnp.concatenate([srct[:, k * nblk:(k + 1) * nblk] for k in range(taps)], axis=0)
        rhs = jnp.concatenate([beam_ref[c, k] for k in range(taps)], axis=1)
        outt = jnp.dot(rhs, stacked, preferred_element_type=jnp.float32)
        out = outt.T
        out_ref[:, c] = out.astype(out_ref.dtype).reshape(out_ref.shape[0], out_ref.shape[2], out_ref.shape[3])

def smooth(sky3, beam, pat_t, parts, first, steps):
    chans, nblk, blk = sky3.shape
    taps = beam.shape[1]
    return pl.pallas_call(
        smooth_kernel,
        out_shape=jax.ShapeDtypeStruct((parts, steps * CT, nblk // parts, blk), jnp.bfloat16),
        grid=(steps,),
        in_specs=[pl.BlockSpec((taps, CT, nblk), lambda i: (0, i + first, 0)),
                  pl.BlockSpec((CT, nblk, blk), lambda i: (i + first, 0, 0)),
                  pl.BlockSpec((CT, taps, blk, blk), lambda i: (i + first, 0, 0, 0))],
        out_specs=pl.BlockSpec((parts, CT, nblk // parts, blk), lambda i: (0, i, 0, 0)),
    )(pat_t, sky3, beam)


HI = lax.Precision.HIGHEST

def build_gram(x, nb, bs, scale):
    n, w = x.shape
    pairs = nb // 2
    per = n // pairs
    span = (nb + 1) * bs
    q = w // span
    size = nb * bs
    mats = []
    for i in range(pairs):
        xi = x[i * per:(i + 1) * per]
        mats.append(jnp.concatenate([xi[:, h * span:(h + 1) * span] for h in range(q)], axis=0))
    rows = []
    for r in range(nb):
        if r < pairs:
            data = mats[r][:, :(nb - r) * bs]
            if r:
                data = jnp.concatenate([jnp.zeros((bs, r * bs), jnp.float32), data], axis=1)
            rows.append(data)
        else:
            rows.append(mats[nb - 1 - r][:, span - size:])
    half = jnp.concatenate(rows, axis=0)
    blk = lax.broadcasted_iota(jnp.int32, (size, size), 0) // bs
    blk_t = lax.broadcasted_iota(jnp.int32, (size, size), 1) // bs
    return jnp.where(blk <= blk_t, half, half.T) * scale


def sweep_kernel(g_ref, b_ref, o_ref, *, iters, nb, bs, scale):
    g = build_gram(g_ref[...], nb, bs, scale)
    bt = b_ref[...]
    m = bt.shape[0]
    rows = lax.broadcasted_iota(jnp.int32, (m, m), 0)
    cols = lax.broadcasted_iota(jnp.int32, (m, m), 1)
    for _ in range(iters):
        it = jnp.dot(bt, g, precision=HI, preferred_element_type=jnp.float32)
        a = lax.dot_general(it, it, (((1,), (1,)), ((), ())), precision=HI,
                            preferred_element_type=jnp.float32)
        rest = jnp.where(rows == cols, 1.0, 0.0).astype(jnp.float32)
        inv = jnp.zeros((m, m), jnp.float32)
        for j in range(m):
            d = jnp.sqrt(a[j:j + 1, j:j + 1])
            col = jnp.where(rows[:, j:j + 1] >= j, a[:, j:j + 1] / d, 0.0)
            row = jnp.where(cols[j:j + 1, :] >= j, a[j:j + 1, :] / d, 0.0)
            a = a - col * row
            r = rest[j:j + 1, :] / d
            inv = jnp.where(rows == j, r, inv)
            rest = rest - col * r
        bad = jnp.isnan(jnp.sum(inv, keepdims=True))
        inv = jnp.where(bad, jnp.nan, inv)
        bt = jnp.dot(inv, it, precision=HI, preferred_element_type=jnp.float32)
    o_ref[...] = bt

def sweeps(packed, basis, iters, nb, bs, scale):
    bt = basis.T
    out = pl.pallas_call(
        functools.partial(sweep_kernel, iters=iters, nb=nb, bs=bs, scale=scale),
        out_shape=jax.ShapeDtypeStruct(bt.shape, jnp.float32),
    )(packed, bt)
    return out.T


def sum_all(pieces):
    n = pieces.shape[0]
    got = lax.all_to_all(pieces, AXES, 0, 0, tiled=False)
    mine = jnp.sum(got, axis=0)
    spread = jnp.broadcast_to(mine[None], (n,) + mine.shape)
    return lax.all_to_all(spread, AXES, 0, 0, tiled=False)


def pack_gram(partial, nb, n):
    size = partial.shape[0]
    bs = size // nb
    pairs = nb // 2
    q = bs * pairs // n
    out = []
    for i in range(pairs):
        k = nb - 1 - i
        m = jnp.concatenate(
            [partial[i * bs:(i + 1) * bs, i * bs:], partial[k * bs:(k + 1) * bs, k * bs:]], axis=1)
        rows = bs // q
        out.append(jnp.concatenate([m[h * rows:(h + 1) * rows] for h in range(q)], axis=1))
    return jnp.concatenate(out, axis=0)


def local(sky_cube, beam_blocks, pattern, start_modes):
    chans = sky_cube.shape[0]
    pix_group = sky_cube.shape[1]
    block_count = pix_group // BLK
    blocks = sky_cube.reshape(chans, block_count, BLK)
    n_chan = lax.axis_size("chan")
    halves = []
    got = []
    pat_t = jnp.transpose(pattern, (2, 0, 1))
    total = chans // CT
    first = (3 * total) // 8
    for lo, steps in ((0, first), (first, total - first)):
        c_part = smooth(blocks, beam_blocks, pat_t, n_chan, lo, steps)
        halves.append(c_part)
        got.append(lax.all_to_all(c_part, "chan", 0, 0, tiled=True))
    chunks = jnp.concatenate(halves, axis=1)
    by_pixel = jnp.concatenate(got, axis=1)
    by_pixel = by_pixel.reshape((n_chan * chans,) + by_pixel.shape[2:])
    all_pixels = pix_group * lax.axis_size("pix")
    basis = start_modes
    partial_value = lax.dot_general(
        by_pixel, by_pixel, (((1, 2), (1, 2)), ((), ())), preferred_element_type=jnp.float32)
    nb = 4
    n_dev = lax.axis_size(AXES)
    packed = sum_all(pack_gram(partial_value, nb, n_dev))
    packed = packed.reshape(n_dev, -1)
    basis = sweeps(packed, basis, ITERS, nb, partial_value.shape[0] // nb, 1.0 / all_pixels)
    modes_low = basis.astype(jnp.bfloat16)
    coeffs = jnp.einsum("cm,cbi->mbi", modes_low, by_pixel, preferred_element_type=jnp.float32).astype(jnp.bfloat16)
    spread = jnp.broadcast_to(coeffs[None], (n_chan,) + coeffs.shape)
    gathered = lax.all_to_all(spread, "chan", 0, 0, tiled=False)
    me = lax.axis_index("chan")
    my_modes = lax.dynamic_slice_in_dim(modes_low, me * chans, chans, axis=0)
    removed = jnp.einsum("cm,jmbi->cjbi", my_modes, gathered, preferred_element_type=jnp.float32)
    cleaned = (chunks.transpose(1, 0, 2, 3).astype(jnp.float32) - removed).astype(jnp.bfloat16)
    cleaned = cleaned.reshape(chans, pix_group)
    return (cleaned, basis)


def solution(mesh):
    return jax.shard_map(
        local,
        mesh=mesh,
        in_specs=(P("chan", "pix"), P("chan", None, None, None), P("chan", None, None), P()),
        out_specs=(P("chan", "pix"), P()),
        check_vma=False,
    )
```

```python
import jax
import jax.numpy as jnp
from jax import lax
from jax.sharding import PartitionSpec as P
import functools
from jax.experimental import pallas as pl

BLK = 128
ITERS = 3
AXES = ("chan", "pix")
CT = 8

def smooth_kernel(pat_ref, sky_ref, beam_ref, out_ref):
    taps = beam_ref.shape[1]
    nblk = sky_ref.shape[1]
    ct = sky_ref.shape[0]
    sub = lax.broadcasted_iota(jnp.int32, (nblk, nblk), 0)
    one = jnp.ones((nblk, nblk), jnp.float32)
    zero = jnp.zeros((nblk, nblk), jnp.float32)
    pat = pat_ref[...]
    for c in range(ct):
        selt = jnp.concatenate(
            [jnp.where(pat[k, c:c + 1, :] == sub, one, zero).astype(jnp.bfloat16) for k in range(taps)], axis=1)
        srct = lax.dot_general(sky_ref[c], selt, (((0,), (0,)), ((), ())),
                               preferred_element_type=jnp.float32).astype(jnp.bfloat16)
        stacked = jnp.concatenate([srct[:, k * nblk:(k + 1) * nblk] for k in range(taps)], axis=0)
        rhs = jnp.concatenate([beam_ref[c, k] for k in range(taps)], axis=1)
        outt = jnp.dot(rhs, stacked, preferred_element_type=jnp.float32)
        out = outt.T
        out_ref[:, c] = out.astype(out_ref.dtype).reshape(out_ref.shape[0], out_ref.shape[2], out_ref.shape[3])

def smooth(sky3, beam, pat_t, parts, first, steps):
    chans, nblk, blk = sky3.shape
    taps = beam.shape[1]
    return pl.pallas_call(
        smooth_kernel,
        out_shape=jax.ShapeDtypeStruct((parts, steps * CT, nblk // parts, blk), jnp.bfloat16),
        grid=(steps,),
        in_specs=[pl.BlockSpec((taps, CT, nblk), lambda i: (0, i + first, 0)),
                  pl.BlockSpec((CT, nblk, blk), lambda i: (i, 0, 0)),
                  pl.BlockSpec((CT, taps, blk, blk), lambda i: (i + first, 0, 0, 0))],
        out_specs=pl.BlockSpec((parts, CT, nblk // parts, blk), lambda i: (0, i, 0, 0)),
    )(pat_t, sky3, beam)


HI = lax.Precision.HIGHEST

def build_gram(x, nb, bs, scale):
    n, w = x.shape
    pairs = nb // 2
    per = n // pairs
    span = (nb + 1) * bs
    q = w // span
    size = nb * bs
    mats = []
    for i in range(pairs):
        xi = x[i * per:(i + 1) * per]
        mats.append(jnp.concatenate([xi[:, h * span:(h + 1) * span] for h in range(q)], axis=0))
    rows = []
    for r in range(nb):
        if r < pairs:
            data = mats[r][:, :(nb - r) * bs]
            if r:
                data = jnp.concatenate([jnp.zeros((bs, r * bs), jnp.float32), data], axis=1)
            rows.append(data)
        else:
            rows.append(mats[nb - 1 - r][:, span - size:])
    half = jnp.concatenate(rows, axis=0)
    blk = lax.broadcasted_iota(jnp.int32, (size, size), 0) // bs
    blk_t = lax.broadcasted_iota(jnp.int32, (size, size), 1) // bs
    return jnp.where(blk <= blk_t, half, half.T) * scale


def sweep_kernel(g_ref, b_ref, o_ref, *, iters, nb, bs, scale):
    g = build_gram(g_ref[...], nb, bs, scale)
    bt = b_ref[...]
    m = bt.shape[0]
    rows = lax.broadcasted_iota(jnp.int32, (m, m), 0)
    cols = lax.broadcasted_iota(jnp.int32, (m, m), 1)
    for _ in range(iters):
        it = jnp.dot(bt, g, precision=HI, preferred_element_type=jnp.float32)
        a = lax.dot_general(it, it, (((1,), (1,)), ((), ())), precision=HI,
                            preferred_element_type=jnp.float32)
        rest = jnp.where(rows == cols, 1.0, 0.0).astype(jnp.float32)
        inv = jnp.zeros((m, m), jnp.float32)
        for j in range(m):
            d = jnp.sqrt(a[j:j + 1, j:j + 1])
            col = jnp.where(rows[:, j:j + 1] >= j, a[:, j:j + 1] / d, 0.0)
            row = jnp.where(cols[j:j + 1, :] >= j, a[j:j + 1, :] / d, 0.0)
            a = a - col * row
            r = rest[j:j + 1, :] / d
            inv = jnp.where(rows == j, r, inv)
            rest = rest - col * r
        bad = jnp.isnan(jnp.sum(inv, keepdims=True))
        inv = jnp.where(bad, jnp.nan, inv)
        bt = jnp.dot(inv, it, precision=HI, preferred_element_type=jnp.float32)
    o_ref[...] = bt

def sweeps(packed, basis, iters, nb, bs, scale):
    bt = basis.T
    out = pl.pallas_call(
        functools.partial(sweep_kernel, iters=iters, nb=nb, bs=bs, scale=scale),
        out_shape=jax.ShapeDtypeStruct(bt.shape, jnp.float32),
    )(packed, bt)
    return out.T


def sum_all(pieces):
    n = pieces.shape[0]
    got = lax.all_to_all(pieces, AXES, 0, 0, tiled=False)
    mine = jnp.sum(got, axis=0)
    spread = jnp.broadcast_to(mine[None], (n,) + mine.shape)
    return lax.all_to_all(spread, AXES, 0, 0, tiled=False)


def pack_gram(partial, nb, n):
    size = partial.shape[0]
    bs = size // nb
    pairs = nb // 2
    q = bs * pairs // n
    out = []
    for i in range(pairs):
        k = nb - 1 - i
        m = jnp.concatenate(
            [partial[i * bs:(i + 1) * bs, i * bs:], partial[k * bs:(k + 1) * bs, k * bs:]], axis=1)
        rows = bs // q
        out.append(jnp.concatenate([m[h * rows:(h + 1) * rows] for h in range(q)], axis=1))
    return jnp.concatenate(out, axis=0)


def local(sky_cube, beam_blocks, pattern, start_modes):
    chans = sky_cube.shape[0]
    pix_group = sky_cube.shape[1]
    block_count = pix_group // BLK
    n_chan = lax.axis_size("chan")
    halves = []
    got = []
    pat_t = jnp.transpose(pattern, (2, 0, 1))
    steps = chans // CT // 2
    for part in range(2):
        lo = part * steps * CT
        own = sky_cube[lo:lo + steps * CT].reshape(steps * CT, block_count, BLK)
        c_part = smooth(own, beam_blocks, pat_t, n_chan, part * steps, steps)
        halves.append(c_part)
        got.append(lax.all_to_all(c_part, "chan", 0, 0, tiled=True))
    chunks = jnp.concatenate(halves, axis=1)
    by_pixel = jnp.concatenate(got, axis=1)
    by_pixel = by_pixel.reshape((n_chan * chans,) + by_pixel.shape[2:])
    all_pixels = pix_group * lax.axis_size("pix")
    basis = start_modes
    partial_value = lax.dot_general(
        by_pixel, by_pixel, (((1, 2), (1, 2)), ((), ())), preferred_element_type=jnp.float32)
    nb = 4
    n_dev = lax.axis_size(AXES)
    packed = sum_all(pack_gram(partial_value, nb, n_dev))
    packed = packed.reshape(n_dev, -1)
    basis = sweeps(packed, basis, ITERS, nb, partial_value.shape[0] // nb, 1.0 / all_pixels)
    modes_low = basis.astype(jnp.bfloat16)
    coeffs = jnp.einsum("cm,cbi->mbi", modes_low, by_pixel, preferred_element_type=jnp.float32).astype(jnp.bfloat16)
    spread = jnp.broadcast_to(coeffs[None], (n_chan,) + coeffs.shape)
    gathered = lax.all_to_all(spread, "chan", 0, 0, tiled=False)
    me = lax.axis_index("chan")
    my_modes = lax.dynamic_slice_in_dim(modes_low, me * chans, chans, axis=0)
    removed = jnp.einsum("cm,jmbi->cjbi", my_modes, gathered, preferred_element_type=jnp.float32)
    cleaned = (chunks.transpose(1, 0, 2, 3).astype(jnp.float32) - removed).astype(jnp.bfloat16)
    cleaned = cleaned.reshape(chans, pix_group)
    return (cleaned, basis)


def solution(mesh):
    return jax.shard_map(
        local,
        mesh=mesh,
        in_specs=(P("chan", "pix"), P("chan", None, None, None), P("chan", None, None), P()),
        out_specs=(P("chan", "pix"), P()),
        check_vma=False,
    )
```

```python
import jax
import jax.numpy as jnp
from jax import lax
from jax.sharding import PartitionSpec as P
import functools
from jax.experimental import pallas as pl

BLK = 128
ITERS = 3
AXES = ("chan", "pix")
CT = 16

def smooth_kernel(pat_ref, sky_ref, beam_ref, out_ref):
    taps = beam_ref.shape[1]
    nblk = sky_ref.shape[1]
    ct = sky_ref.shape[0]
    sub = lax.broadcasted_iota(jnp.int32, (nblk, nblk), 0)
    one = jnp.ones((nblk, nblk), jnp.float32)
    zero = jnp.zeros((nblk, nblk), jnp.float32)
    pat = pat_ref[...]
    for c in range(ct):
        selt = jnp.concatenate(
            [jnp.where(pat[k, c:c + 1, :] == sub, one, zero).astype(jnp.bfloat16) for k in range(taps)], axis=1)
        srct = lax.dot_general(sky_ref[c], selt, (((0,), (0,)), ((), ())),
                               preferred_element_type=jnp.float32).astype(jnp.bfloat16)
        stacked = jnp.concatenate([srct[:, k * nblk:(k + 1) * nblk] for k in range(taps)], axis=0)
        rhs = jnp.concatenate([beam_ref[c, k] for k in range(taps)], axis=1)
        outt = jnp.dot(rhs, stacked, preferred_element_type=jnp.float32)
        out = outt.T
        out_ref[:, c] = out.astype(out_ref.dtype).reshape(out_ref.shape[0], out_ref.shape[2], out_ref.shape[3])

def smooth(sky3, beam, pat_t, parts, first, steps):
    chans, nblk, blk = sky3.shape
    taps = beam.shape[1]
    return pl.pallas_call(
        smooth_kernel,
        out_shape=jax.ShapeDtypeStruct((parts, steps * CT, nblk // parts, blk), jnp.bfloat16),
        grid=(steps,),
        in_specs=[pl.BlockSpec((taps, CT, nblk), lambda i: (0, i + first, 0)),
                  pl.BlockSpec((CT, nblk, blk), lambda i: (i, 0, 0)),
                  pl.BlockSpec((CT, taps, blk, blk), lambda i: (i + first, 0, 0, 0))],
        out_specs=pl.BlockSpec((parts, CT, nblk // parts, blk), lambda i: (0, i, 0, 0)),
    )(pat_t, sky3, beam)


HI = lax.Precision.HIGHEST

def build_gram(x, nb, bs, scale):
    n, w = x.shape
    pairs = nb // 2
    per = n // pairs
    span = (nb + 1) * bs
    q = w // span
    size = nb * bs
    mats = []
    for i in range(pairs):
        xi = x[i * per:(i + 1) * per]
        mats.append(jnp.concatenate([xi[:, h * span:(h + 1) * span] for h in range(q)], axis=0))
    rows = []
    for r in range(nb):
        if r < pairs:
            data = mats[r][:, :(nb - r) * bs]
            if r:
                data = jnp.concatenate([jnp.zeros((bs, r * bs), jnp.float32), data], axis=1)
            rows.append(data)
        else:
            rows.append(mats[nb - 1 - r][:, span - size:])
    half = jnp.concatenate(rows, axis=0)
    blk = lax.broadcasted_iota(jnp.int32, (size, size), 0) // bs
    blk_t = lax.broadcasted_iota(jnp.int32, (size, size), 1) // bs
    return jnp.where(blk <= blk_t, half, half.T) * scale


def sweep_kernel(g_ref, b_ref, o_ref, *, iters, nb, bs, scale):
    g = build_gram(g_ref[...], nb, bs, scale)
    bt = b_ref[...]
    m = bt.shape[0]
    rows = lax.broadcasted_iota(jnp.int32, (m, m), 0)
    cols = lax.broadcasted_iota(jnp.int32, (m, m), 1)
    for _ in range(iters):
        it = jnp.dot(bt, g, precision=HI, preferred_element_type=jnp.float32)
        a = lax.dot_general(it, it, (((1,), (1,)), ((), ())), precision=HI,
                            preferred_element_type=jnp.float32)
        rest = jnp.where(rows == cols, 1.0, 0.0).astype(jnp.float32)
        inv = jnp.zeros((m, m), jnp.float32)
        for j in range(m):
            d = jnp.sqrt(a[j:j + 1, j:j + 1])
            col = jnp.where(rows[:, j:j + 1] >= j, a[:, j:j + 1] / d, 0.0)
            row = jnp.where(cols[j:j + 1, :] >= j, a[j:j + 1, :] / d, 0.0)
            a = a - col * row
            r = rest[j:j + 1, :] / d
            inv = jnp.where(rows == j, r, inv)
            rest = rest - col * r
        bad = jnp.isnan(jnp.sum(inv, keepdims=True))
        inv = jnp.where(bad, jnp.nan, inv)
        bt = jnp.dot(inv, it, precision=HI, preferred_element_type=jnp.float32)
    o_ref[...] = bt

def sweeps(packed, basis, iters, nb, bs, scale):
    bt = basis.T
    out = pl.pallas_call(
        functools.partial(sweep_kernel, iters=iters, nb=nb, bs=bs, scale=scale),
        out_shape=jax.ShapeDtypeStruct(bt.shape, jnp.float32),
    )(packed, bt)
    return out.T


def sum_all(pieces):
    n = pieces.shape[0]
    got = lax.all_to_all(pieces, AXES, 0, 0, tiled=False)
    mine = jnp.sum(got, axis=0)
    spread = jnp.broadcast_to(mine[None], (n,) + mine.shape)
    return lax.all_to_all(spread, AXES, 0, 0, tiled=False)


def pack_gram(partial, nb, n):
    size = partial.shape[0]
    bs = size // nb
    pairs = nb // 2
    q = bs * pairs // n
    out = []
    for i in range(pairs):
        k = nb - 1 - i
        m = jnp.concatenate(
            [partial[i * bs:(i + 1) * bs, i * bs:], partial[k * bs:(k + 1) * bs, k * bs:]], axis=1)
        rows = bs // q
        out.append(jnp.concatenate([m[h * rows:(h + 1) * rows] for h in range(q)], axis=1))
    return jnp.concatenate(out, axis=0)


def local(sky_cube, beam_blocks, pattern, start_modes):
    chans = sky_cube.shape[0]
    pix_group = sky_cube.shape[1]
    block_count = pix_group // BLK
    n_chan = lax.axis_size("chan")
    halves = []
    got = []
    pat_t = jnp.transpose(pattern, (2, 0, 1))
    steps = chans // CT // 2
    for part in range(2):
        lo = part * steps * CT
        own = sky_cube[lo:lo + steps * CT].reshape(steps * CT, block_count, BLK)
        c_part = smooth(own, beam_blocks, pat_t, n_chan, part * steps, steps)
        halves.append(c_part)
        got.append(lax.all_to_all(c_part, "chan", 0, 0, tiled=True))
    chunks = jnp.concatenate(halves, axis=1)
    by_pixel = jnp.concatenate(got, axis=1)
    by_pixel = by_pixel.reshape((n_chan * chans,) + by_pixel.shape[2:])
    all_pixels = pix_group * lax.axis_size("pix")
    basis = start_modes
    partial_value = lax.dot_general(
        by_pixel, by_pixel, (((1, 2), (1, 2)), ((), ())), preferred_element_type=jnp.float32)
    nb = 4
    n_dev = lax.axis_size(AXES)
    packed = sum_all(pack_gram(partial_value, nb, n_dev))
    packed = packed.reshape(n_dev, -1)
    basis = sweeps(packed, basis, ITERS, nb, partial_value.shape[0] // nb, 1.0 / all_pixels)
    modes_low = basis.astype(jnp.bfloat16)
    coeffs = jnp.einsum("cm,cbi->mbi", modes_low, by_pixel, preferred_element_type=jnp.float32).astype(jnp.bfloat16)
    spread = jnp.broadcast_to(coeffs[None], (n_chan,) + coeffs.shape)
    gathered = lax.all_to_all(spread, "chan", 0, 0, tiled=False)
    me = lax.axis_index("chan")
    my_modes = lax.dynamic_slice_in_dim(modes_low, me * chans, chans, axis=0)
    removed = jnp.einsum("cm,jmbi->cjbi", my_modes, gathered, preferred_element_type=jnp.float32)
    cleaned = (chunks.transpose(1, 0, 2, 3).astype(jnp.float32) - removed).astype(jnp.bfloat16)
    cleaned = cleaned.reshape(chans, pix_group)
    return (cleaned, basis)


def solution(mesh):
    return jax.shard_map(
        local,
        mesh=mesh,
        in_specs=(P("chan", "pix"), P("chan", None, None, None), P("chan", None, None), P()),
        out_specs=(P("chan", "pix"), P()),
        check_vma=False,
    )
```

```python
import jax
import jax.numpy as jnp
from jax import lax
from jax.sharding import PartitionSpec as P
import functools
from jax.experimental import pallas as pl

BLK = 128
ITERS = 3
AXES = ("chan", "pix")
CT = 8

def smooth_kernel(pat_ref, sky_ref, beam_ref, out_ref):
    taps = beam_ref.shape[1]
    nblk = sky_ref.shape[1]
    ct = sky_ref.shape[0]
    sub = lax.broadcasted_iota(jnp.int32, (nblk, nblk), 0)
    one = jnp.ones((nblk, nblk), jnp.float32)
    zero = jnp.zeros((nblk, nblk), jnp.float32)
    pat = pat_ref[...]
    for c in range(ct):
        selt = jnp.concatenate(
            [jnp.where(pat[k, c:c + 1, :] == sub, one, zero).astype(jnp.bfloat16) for k in range(taps)], axis=1)
        srct = lax.dot_general(sky_ref[c], selt, (((0,), (0,)), ((), ())),
                               preferred_element_type=jnp.float32).astype(jnp.bfloat16)
        stacked = jnp.concatenate([srct[:, k * nblk:(k + 1) * nblk] for k in range(taps)], axis=0)
        rhs = jnp.concatenate([beam_ref[c, k] for k in range(taps)], axis=1)
        outt = jnp.dot(rhs, stacked, preferred_element_type=jnp.float32)
        out = outt.T
        out_ref[:, c] = out.astype(out_ref.dtype).reshape(out_ref.shape[0], out_ref.shape[2], out_ref.shape[3])

def smooth(sky3, beam, pat_t, parts, first, steps):
    chans, nblk, blk = sky3.shape
    taps = beam.shape[1]
    return pl.pallas_call(
        smooth_kernel,
        out_shape=jax.ShapeDtypeStruct((parts, steps * CT, nblk // parts, blk), jnp.bfloat16),
        grid=(steps,),
        in_specs=[pl.BlockSpec((taps, CT, nblk), lambda i: (0, i + first, 0)),
                  pl.BlockSpec((CT, nblk, blk), lambda i: (i, 0, 0)),
                  pl.BlockSpec((CT, taps, blk, blk), lambda i: (i + first, 0, 0, 0))],
        out_specs=pl.BlockSpec((parts, CT, nblk // parts, blk), lambda i: (0, i, 0, 0)),
    )(pat_t, sky3, beam)


HI = lax.Precision.HIGHEST

def build_gram(x, nb, bs, scale):
    n, w = x.shape
    pairs = nb // 2
    per = n // pairs
    span = (nb + 1) * bs
    q = w // span
    size = nb * bs
    mats = []
    for i in range(pairs):
        xi = x[i * per:(i + 1) * per]
        mats.append(jnp.concatenate([xi[:, h * span:(h + 1) * span] for h in range(q)], axis=0))
    rows = []
    for r in range(nb):
        if r < pairs:
            data = mats[r][:, :(nb - r) * bs]
            if r:
                data = jnp.concatenate([jnp.zeros((bs, r * bs), jnp.float32), data], axis=1)
            rows.append(data)
        else:
            rows.append(mats[nb - 1 - r][:, span - size:])
    half = jnp.concatenate(rows, axis=0)
    blk = lax.broadcasted_iota(jnp.int32, (size, size), 0) // bs
    blk_t = lax.broadcasted_iota(jnp.int32, (size, size), 1) // bs
    return jnp.where(blk <= blk_t, half, half.T) * scale


def sweep_kernel(g_ref, b_ref, o_ref, low_ref, *, iters, nb, bs, scale):
    g = build_gram(g_ref[...], nb, bs, scale)
    bt = b_ref[...]
    m = bt.shape[0]
    rows = lax.broadcasted_iota(jnp.int32, (m, m), 0)
    cols = lax.broadcasted_iota(jnp.int32, (m, m), 1)
    for _ in range(iters):
        it = jnp.dot(bt, g, precision=HI, preferred_element_type=jnp.float32)
        a = lax.dot_general(it, it, (((1,), (1,)), ((), ())), precision=HI,
                            preferred_element_type=jnp.float32)
        rest = jnp.where(rows == cols, 1.0, 0.0).astype(jnp.float32)
        inv = jnp.zeros((m, m), jnp.float32)
        for j in range(m):
            d = jnp.sqrt(a[j:j + 1, j:j + 1])
            col = jnp.where(rows[:, j:j + 1] >= j, a[:, j:j + 1] / d, 0.0)
            row = jnp.where(cols[j:j + 1, :] >= j, a[j:j + 1, :] / d, 0.0)
            a = a - col * row
            r = rest[j:j + 1, :] / d
            inv = jnp.where(rows == j, r, inv)
            rest = rest - col * r
        bad = jnp.isnan(jnp.sum(inv, keepdims=True))
        inv = jnp.where(bad, jnp.nan, inv)
        bt = jnp.dot(inv, it, precision=HI, preferred_element_type=jnp.float32)
    o_ref[...] = bt
    low_ref[...] = bt.astype(low_ref.dtype)

def sweeps(packed, basis, iters, nb, bs, scale):
    bt = basis.T
    out, low = pl.pallas_call(
        functools.partial(sweep_kernel, iters=iters, nb=nb, bs=bs, scale=scale),
        out_shape=(jax.ShapeDtypeStruct(bt.shape, jnp.float32),
                   jax.ShapeDtypeStruct(bt.shape, jnp.bfloat16)),
    )(packed, bt)
    return out.T, low


def sum_all(pieces):
    n = pieces.shape[0]
    got = lax.all_to_all(pieces, AXES, 0, 0, tiled=False)
    mine = jnp.sum(got, axis=0)
    spread = jnp.broadcast_to(mine[None], (n,) + mine.shape)
    return lax.all_to_all(spread, AXES, 0, 0, tiled=False)


def pack_gram(partial, nb, n):
    size = partial.shape[0]
    bs = size // nb
    pairs = nb // 2
    q = bs * pairs // n
    out = []
    for i in range(pairs):
        k = nb - 1 - i
        m = jnp.concatenate(
            [partial[i * bs:(i + 1) * bs, i * bs:], partial[k * bs:(k + 1) * bs, k * bs:]], axis=1)
        rows = bs // q
        out.append(jnp.concatenate([m[h * rows:(h + 1) * rows] for h in range(q)], axis=1))
    return jnp.concatenate(out, axis=0)


def local(sky_cube, beam_blocks, pattern, start_modes):
    chans = sky_cube.shape[0]
    pix_group = sky_cube.shape[1]
    block_count = pix_group // BLK
    n_chan = lax.axis_size("chan")
    halves = []
    got = []
    pat_t = jnp.transpose(pattern, (2, 0, 1))
    steps = chans // CT // 2
    for part in range(2):
        lo = part * steps * CT
        own = sky_cube[lo:lo + steps * CT].reshape(steps * CT, block_count, BLK)
        c_part = smooth(own, beam_blocks, pat_t, n_chan, part * steps, steps)
        halves.append(c_part)
        got.append(lax.all_to_all(c_part, "chan", 0, 0, tiled=True))
    chunks = jnp.concatenate(halves, axis=1)
    by_pixel = jnp.concatenate(got, axis=1)
    by_pixel = by_pixel.reshape((n_chan * chans,) + by_pixel.shape[2:])
    all_pixels = pix_group * lax.axis_size("pix")
    basis = start_modes
    partial_value = lax.dot_general(
        by_pixel, by_pixel, (((1, 2), (1, 2)), ((), ())), preferred_element_type=jnp.float32)
    nb = 4
    n_dev = lax.axis_size(AXES)
    packed = sum_all(pack_gram(partial_value, nb, n_dev))
    packed = packed.reshape(n_dev, -1)
    basis, modes_t = sweeps(packed, basis, ITERS, nb, partial_value.shape[0] // nb, 1.0 / all_pixels)
    coeffs = jnp.einsum("mc,cbi->mbi", modes_t, by_pixel, preferred_element_type=jnp.float32).astype(jnp.bfloat16)
    spread = jnp.broadcast_to(coeffs[None], (n_chan,) + coeffs.shape)
    gathered = lax.all_to_all(spread, "chan", 0, 0, tiled=False)
    me = lax.axis_index("chan")
    my_modes = lax.dynamic_slice_in_dim(modes_t, me * chans, chans, axis=1)
    removed = jnp.einsum("mc,jmbi->cjbi", my_modes, gathered, preferred_element_type=jnp.float32)
    cleaned = (chunks.transpose(1, 0, 2, 3).astype(jnp.float32) - removed).astype(jnp.bfloat16)
    cleaned = cleaned.reshape(chans, pix_group)
    return (cleaned, basis)


def solution(mesh):
    return jax.shard_map(
        local,
        mesh=mesh,
        in_specs=(P("chan", "pix"), P("chan", None, None, None), P("chan", None, None), P()),
        out_specs=(P("chan", "pix"), P()),
        check_vma=False,
    )
```
